128 devices in a mesh: tok: 16 (over z, y), head: 8 (over x, core).
Axes of the slice: x: 4, y: 4, z: 4, core: 2. Of those that a mesh axis runs over, the one named last changes fastest.
Arguments:
- hidden_in: bfloat16 [16384, 2048], P(('tok', 'head')), may hold values from -6 to 6
- context_len: int32 [16], P('tok'), may hold values from 1 to 2048, 16384 in all
- page_table: int32 [16, 16], P('tok'), may hold values from 0 to 15, as said below
- paged_cache: bfloat16 [2, 256, 128, 2048], P(None, 'tok', None, 'head'), may hold values from -139 to 139
- attn_gain: bfloat16 [2048], replicated, may hold values from 0.5 to 1.5
- proj_weight: bfloat16 [3, 2048, 2048], P(None, None, 'head'), may hold values from -0.125 to 0.125
- proj_bias: bfloat16 [3, 2048], P(None, 'head'), may hold values from -3 to 3
- out_weight: bfloat16 [2048, 2048], P('head'), may hold values from -0.125 to 0.125
- mlp_gain: bfloat16 [2048], replicated, may hold values from 0.5 to 1.5
- expert_ids: int32 [16384, 4], P(('tok', 'head')), may hold values from 0 to 63, all different within a row; in each aligned block of 128 rows (0 to 127, 128 to 255, ...) at most 10 rows name the same one
- route_weight: float32 [16384, 4], P(('tok', 'head')), may hold values from 0.05 to 0.5
- w_experts_in: bfloat16 [128, 2048, 1408], P(('tok', 'head')), may hold values from -0.125 to 0.125
- w_experts_out: bfloat16 [128, 704, 2048], P(('tok', 'head')), may hold values from -0.15625 to 0.15625
- w_shared_in: bfloat16 [2048, 2, 5632], P(None, None, 'head'), may hold values from -0.125 to 0.125
- w_shared_out: bfloat16 [5632, 2048], P('head'), may hold values from -0.078125 to 0.078125
- shared_gate: bfloat16 [2048], replicated, may hold values from -0.125 to 0.125
Outputs:
- layer_out: bfloat16 [16384, 2048], P(('tok', 'head'))
The draws below stay inside these ranges and needn't reach their ends.
Inputs may be any that keep to these rules, and one draw needn't show every extreme that they name: `page_table`: each row is a permutation of the pool's pages. `context_len`: some request has exactly 2048 cached tokens. `expert_ids`: the experts of a row differ; within the 128 rows of one device no expert is named more than 10 times, a bound that some block reaches.
All inputs are finite; a program needn't handle non-finite values. No bound on the sum of `context_len` on one device may be relied on, other than what follows from the above.
Results may differ from the reference program's by a relative error of at most 0.02.
Values may be sent and summed in bfloat16 or wider, within the bound.
No kernel may reach another device: no remote copies, remote signals or barrier semaphores. Data moves between devices by JAX's collectives and lax.ppermute only.
A program may use at most 128 MiB of HBM per device.

```python
import math
import jax
import jax.numpy as jnp
import numpy as np
from jax import lax

D = 2048
HEADS = 16
HD = 128
MOE_FF = 1408
SHARED_FF = 5632
TOP = 4
TOK_DEV = 128
CTX = 2048
PAGE = 128
EXPERTS = 64
HALF = 704
CAP = 10
REQS = 16
STRETCH = 1024
TOKENS = 16384
PAGES_DEV = 16
N_TOK = 16
N_HEAD = 8


def draw_page_table(key, part):
    subkeys = jax.random.split(key, REQS)

    def single_row(subkey):
        return jax.random.permutation(subkey, PAGES_DEV)
    return jax.vmap(single_row)(subkeys).astype(jnp.int32)


def draw_paged_cache(key, part):
    shape = (2, REQS * PAGES_DEV, PAGE, HEADS * HD)
    base = jnp.clip(jax.random.normal(key, shape, jnp.float32), -6.0, 6.0)
    return base.astype(jnp.bfloat16)


def shard_levels(key, dims, cuts, smallest, top_value):
    level, own = 1.0, jax.random.fold_in(key, 6)
    for dim, parts in cuts:
        steps = jnp.exp(jax.random.uniform(jax.random.fold_in(own, dim), (parts,), jnp.float32, smallest / len(cuts), top_value / len(cuts)))
        level = level * jnp.repeat(steps, dims[dim] // parts).reshape([-1 if axis == dim else 1 for axis in range(len(dims))])
    return level


def split_up(amount, total, bound, lean):
    loads = [(1 << 20) // math.isqrt(rank ** lean) + 1 for rank in range(2, amount + 1)]
    spare, given = total - bound - (amount - 1), [1] * (amount - 1)
    while spare > 0:
        candidates = [i for i in range(amount - 1) if given[i] < bound]
        whole, remaining = sum([loads[i] for i in candidates]), spare
        for i in candidates:
            addition = min(bound - given[i], max(1, remaining * loads[i] // whole), spare)
            given[i] = given[i] + addition
            spare = spare - addition
    return np.array([bound] + given)


def ragged(key, count, total, reach, skew):
    if count == 2:
        one = jax.random.randint(key, (), max(1, total - reach), min(reach, total - 1) + 1)
        return jnp.stack([one, total - one])
    sizes = jnp.asarray(split_up(count, total, reach, skew), jnp.int32)
    twos = (count - 1) // 2
    source_of, sink = sizes[1:1 + 2 * twos:2], sizes[2:2 + 2 * twos:2]
    margin = jnp.minimum(source_of - 1, reach - sink)
    passed = jax.random.randint(jax.random.fold_in(key, 1), (twos,), 0, 1 << 20) % (margin + 1)
    sizes = sizes.at[1:1 + 2 * twos:2].set(source_of - passed).at[2:2 + 2 * twos:2].set(sink + passed)
    return sizes[jax.random.permutation(jax.random.fold_in(key, 2), count)]


def deal_out(stream_key, own, number, rows, amount, top, most, lean):
    sequence = jax.random.permutation(stream_key, amount)
    crowded, common = portions_of(amount, rows * top, most, lean, True), portions_of(amount, rows * top, most, lean, False)
    places = jnp.arange(amount)

    def named(sizes, offset_by):
        used = int((sizes > 0).sum())
        fixed = max(1, used // 4)
        shifted = fixed + (places - fixed + offset_by * (used - fixed)) % max(1, amount - fixed)
        return jnp.zeros((amount,), jnp.int32).at[sequence[jnp.where(places < fixed, places, shifted)]].set(jnp.asarray(sizes, jnp.int32))

    sizes = jnp.where(number % 4 == 0, named(crowded, number // 4), named(common, number - number // 4 - 1))
    mixed = jax.random.permutation(jax.random.fold_in(own, 3), amount)
    donor, sink = mixed[0:amount // 2 * 2:2], mixed[1:amount // 2 * 2:2]
    room = jnp.minimum(sizes[donor] - 1, most - sizes[sink]) // 2
    room = jnp.where((donor == sequence[0]) | (sink == sequence[0]) | (sizes[sink] == 0), 0, jnp.maximum(room, 0))
    shifted = jax.random.randint(jax.random.fold_in(own, 4), (amount // 2,), 0, 1 << 20) % (room + 1)
    sizes = sizes.at[donor].add(-shifted).at[sink].add(shifted)
    items = jnp.searchsorted(jnp.cumsum(sizes), jnp.arange(rows * top), side="right").astype(jnp.int32)
    listing = items.reshape(top, rows).T
    listing = listing[jax.random.permutation(jax.random.fold_in(own, 1), rows)]
    offset_by = jax.random.randint(jax.random.fold_in(own, 2), (rows, 1), 0, top)
    return jnp.take_along_axis(listing, (jnp.arange(top)[None, :] + offset_by) % top, axis=1)


def portions_of(count, total, most, slope, full):
    portions = [(1 << 20) // math.isqrt(standing ** slope) + 1 for standing in range(1, count + 1)]
    largest = most if full else min(most, max(-(-total // count), total * portions[0] // sum(portions)))
    least = 1 if total - largest >= count - 1 else 0
    given, surplus = [largest] + [least] * (count - 1), total - largest - least * (count - 1)
    while surplus > 0:
        movable = [i for i in range(1, count) if given[i] < largest] or [i for i in range(1, count) if given[i] < most]
        whole, left = sum([portions[i] for i in movable]), surplus
        for i in movable:
            extra = min(most - given[i], max(1, left * portions[i] // whole), surplus)
            given[i] = given[i] + extra
            surplus = surplus - extra
    return np.array(given)


def gaussian(own_key, shape, scale, bound, cuts=(), kind=jnp.bfloat16):
    values = scale * jax.random.normal(own_key, shape, jnp.float32)
    if cuts:
        values = values * shard_levels(own_key, shape, cuts, -0.22, 0.18)
    return jnp.clip(values, -bound, bound).astype(kind)


def setup_inputs(seed: int = 0) -> dict:
    splits = jax.random.split(jax.random.key(seed), 17)
    hidden_in = gaussian(splits[0], (TOKENS, D), 1.0, 6.0, ((0, 128),))
    context_len = ragged(splits[1], REQS, REQS * CTX // 2, CTX, 1).astype(jnp.int32)
    page_table = draw_page_table(jax.random.fold_in(splits[16], 71), 0)
    paged_cache = draw_paged_cache(jax.random.fold_in(splits[16], 71), 0)
    attn_gain = jnp.clip(1.0 + 0.1 * jax.random.normal(splits[4], (D,), jnp.float32), 0.5, 1.5).astype(jnp.bfloat16)
    proj_weight = gaussian(splits[5], (3, D, HEADS * HD), D ** -0.5, 0.125, ((2, 8),))
    proj_bias = gaussian(splits[6], (3, HEADS * HD), 0.5, 3.0, ((1, 8),))
    out_weight = gaussian(splits[7], (HEADS * HD, D), (HEADS * HD) ** -0.5, 0.125, ((0, 8),))
    mlp_gain = jnp.clip(1.0 + 0.1 * jax.random.normal(splits[8], (D,), jnp.float32), 0.5, 1.5).astype(jnp.bfloat16)
    expert_ids_keys = jax.random.split(jax.random.fold_in(splits[9], 1), TOKENS // TOK_DEV)
    expert_ids_turns = jax.random.permutation(jax.random.fold_in(splits[9], 3), TOKENS // TOK_DEV)
    expert_ids = jax.vmap(lambda own, number: deal_out(jax.random.fold_in(splits[9], 2), own, number, TOK_DEV, EXPERTS, TOP, CAP, 2))(expert_ids_keys, expert_ids_turns).reshape((TOKENS, TOP))
    route_weight = jnp.clip(0.05 + 0.45 * jax.random.uniform(splits[10], (TOKENS, TOP), jnp.float32) ** shard_levels(splits[10], (TOKENS, TOP), ((0, 128),), -0.2, 0.2), 0.05, 0.5)
    w_experts_in = gaussian(splits[11], (EXPERTS * 2, D, MOE_FF), D ** -0.5, 0.125, ((0, 128),))
    w_experts_out = gaussian(splits[12], (EXPERTS * 2, HALF, D), MOE_FF ** -0.5, 0.15625, ((0, 128),))
    w_shared_in = gaussian(splits[13], (D, 2, SHARED_FF), D ** -0.5, 0.125, ((2, 8),))
    w_shared_out = gaussian(splits[14], (SHARED_FF, D), SHARED_FF ** -0.5, 0.078125, ((0, 8),))
    shared_gate = gaussian(splits[15], (D,), D ** -0.5, 0.125)
    return {"hidden_in": hidden_in, "context_len": context_len, "page_table": page_table, "paged_cache": paged_cache, "attn_gain": attn_gain, "proj_weight": proj_weight, "proj_bias": proj_bias, "out_weight": out_weight, "mlp_gain": mlp_gain, "expert_ids": expert_ids, "route_weight": route_weight, "w_experts_in": w_experts_in, "w_experts_out": w_experts_out, "w_shared_in": w_shared_in, "w_shared_out": w_shared_out, "shared_gate": shared_gate}


EPS = 1e-06
THETA = 1000000.0

def rms_scale(values, gain):
    wide = values.astype(jnp.float32)
    spread = lax.optimization_barrier(jnp.mean(wide * wide, axis=-1, keepdims=True))
    return (wide * lax.rsqrt(spread + EPS) * gain.astype(jnp.float32)).astype(jnp.bfloat16)

def rotate(vectors, positions):
    middle = vectors.shape[-1] // 2
    frequency = THETA ** (-(jnp.arange(middle, dtype=jnp.float32) * 2.0 / vectors.shape[-1]))
    angles = positions.astype(jnp.float32)[:, None] * frequency[None, :]
    angles = jnp.concatenate([angles, angles], axis=-1)[:, None, :]
    turned = jnp.concatenate([-vectors[..., middle:], vectors[..., :middle]], axis=-1)
    return vectors * jnp.cos(angles) + turned * jnp.sin(angles)

def attend(queries, keys_all, values_all, context, span_len):
    row_count = queries.shape[0]
    head_count = queries.shape[1]
    head_size = queries.shape[2]
    block_rows = math.gcd(row_count, 512)
    block_count = row_count // block_rows
    scale = 1.0 / math.sqrt(head_size)
    key_pos = jnp.arange(keys_all.shape[0], dtype=jnp.int32)
    keys_wide = keys_all.astype(jnp.float32)
    values_wide = values_all.astype(jnp.float32)

    def one_block(items):
        query_block, start = items
        scores = jnp.einsum('qhd,khd->hqk', query_block.astype(jnp.float32), keys_wide) * scale
        query_pos = start + jnp.arange(block_rows, dtype=jnp.int32)
        allowed = jnp.where(key_pos[None, :] < span_len, key_pos[None, :] < context, key_pos[None, :] - span_len <= query_pos[:, None])
        scores = jnp.where(allowed[None], scores, -1e+30)
        largest = lax.optimization_barrier(jnp.max(scores, axis=-1, keepdims=True))
        weights = jnp.where(allowed[None], jnp.exp(scores - largest), 0.0)
        probs = (weights / lax.optimization_barrier(jnp.sum(weights, axis=-1, keepdims=True))).astype(jnp.bfloat16)
        return jnp.einsum('hqk,khd->qhd', probs.astype(jnp.float32), values_wide).astype(jnp.bfloat16)
    starts = jnp.arange(block_count, dtype=jnp.int32) * block_rows
    result = lax.map(one_block, (queries.reshape(block_count, block_rows, head_count, head_size), starts))
    return result.reshape(row_count, head_count, head_size)

def reference(hidden_in, context_len, page_table, paged_cache, attn_gain, proj_weight, proj_bias, out_weight, mlp_gain, expert_ids, route_weight, w_experts_in, w_experts_out, w_shared_in, w_shared_out, shared_gate):
    normed = rms_scale(hidden_in, attn_gain)
    positions = jnp.repeat(context_len, STRETCH) + jnp.tile(jnp.arange(STRETCH, dtype=jnp.int32), REQS)
    projected = jnp.einsum('td,cdf->ctf', normed.astype(jnp.float32), proj_weight.astype(jnp.float32)) + proj_bias.astype(jnp.float32)[:, None, :]
    queries = rotate(projected[0].reshape(TOKENS, HEADS, HD), positions).astype(jnp.bfloat16)
    new_keys = rotate(projected[1].reshape(TOKENS, HEADS, HD), positions).astype(jnp.bfloat16)
    new_values = projected[2].reshape(TOKENS, HEADS, HD).astype(jnp.bfloat16)
    pools = jnp.moveaxis(paged_cache.reshape(2, REQS, PAGES_DEV, PAGE, HEADS * HD), 1, 0)

    def per_request(items):
        query_rows, key_rows, value_rows, pool, table, context = items
        ordered = jnp.take(pool, table, axis=1).reshape(2, CTX, HEADS, HD)
        keys_all = jnp.concatenate([ordered[0], key_rows], axis=0)
        values_all = jnp.concatenate([ordered[1], value_rows], axis=0)
        return attend(query_rows, keys_all, values_all, context, CTX)
    heads_out = lax.map(per_request, (queries.reshape(REQS, STRETCH, HEADS, HD), new_keys.reshape(REQS, STRETCH, HEADS, HD), new_values.reshape(REQS, STRETCH, HEADS, HD), pools, page_table, context_len))
    group_width = HEADS // N_HEAD * HD
    heads_grouped = jnp.moveaxis(heads_out.reshape(TOKENS, N_HEAD, group_width), 1, 0)
    out_weights = out_weight.reshape(N_HEAD, group_width, D)

    def attn_group(total, pieces):
        rows_group, weight_group = pieces
        partial_value = jnp.dot(rows_group, weight_group, preferred_element_type=jnp.float32).astype(jnp.bfloat16)
        return (total + lax.optimization_barrier(partial_value).astype(jnp.float32), None)
    attn_sum = lax.scan(attn_group, jnp.zeros((TOKENS, D), jnp.float32), (heads_grouped, out_weights))[0]
    resid = (hidden_in.astype(jnp.float32) + attn_sum).astype(jnp.bfloat16)
    mixed = rms_scale(resid, mlp_gain)
    shared_width = SHARED_FF // N_HEAD
    shared_in = jnp.transpose(w_shared_in.reshape(D, 2, N_HEAD, shared_width), (2, 0, 1, 3))
    shared_out = w_shared_out.reshape(N_HEAD, shared_width, D)
    mixed_wide = mixed.astype(jnp.float32)

    def shared_group(total, pieces):
        weight_in, weight_out = pieces
        inner = jnp.einsum('td,dcf->tcf', mixed_wide, weight_in.astype(jnp.float32))
        activated = (jax.nn.silu(inner[:, 0]) * inner[:, 1]).astype(jnp.bfloat16)
        partial_value = jnp.dot(activated, weight_out, preferred_element_type=jnp.float32).astype(jnp.bfloat16)
        return (total + lax.optimization_barrier(partial_value).astype(jnp.float32), None)
    shared = lax.scan(shared_group, jnp.zeros((TOKENS, D), jnp.float32), (shared_in, shared_out))[0]
    gate = jax.nn.sigmoid(jnp.dot(mixed, shared_gate, preferred_element_type=jnp.float32))
    copies = TOKENS * TOP
    limit = N_TOK * N_HEAD * CAP
    flat_ids = expert_ids.reshape(-1)
    padded = jnp.concatenate([mixed, jnp.zeros((1, D), jnp.bfloat16)], axis=0)
    weight_pad = jnp.concatenate([route_weight.reshape(-1), jnp.zeros((1,), jnp.float32)])

    def per_expert(total, expert):
        chosen = jnp.nonzero(flat_ids == expert, size=limit, fill_value=copies)[0].astype(jnp.int32)
        token_index = chosen // TOP
        picked = padded[token_index]
        weights = weight_pad[chosen]
        result = jnp.zeros((limit, D), jnp.float32)
        for half_index in range(2):
            weight_row = 2 * expert + half_index
            inner = jnp.dot(picked, w_experts_in[weight_row], preferred_element_type=jnp.float32)
            activated = (jax.nn.silu(inner[:, :HALF]) * inner[:, HALF:]).astype(jnp.bfloat16)
            partial_value = jnp.dot(activated, w_experts_out[weight_row], preferred_element_type=jnp.float32).astype(jnp.bfloat16)
            result = result + lax.optimization_barrier(partial_value).astype(jnp.float32)
        merged = lax.optimization_barrier(result.astype(jnp.bfloat16)).astype(jnp.float32)
        return (total.at[token_index].add(weights[:, None] * merged), None)
    routed = lax.scan(per_expert, jnp.zeros((TOKENS + 1, D), jnp.float32), jnp.arange(EXPERTS, dtype=jnp.int32))[0][:TOKENS]
    return (resid.astype(jnp.float32) + gate[:, None] * shared + routed).astype(jnp.bfloat16)
```

```python
import math

import jax
import jax.numpy as jnp
from jax import lax
from jax.sharding import Mesh, PartitionSpec as P

HD = 128
HEAD = ("x", "core")
ROWS = ("tok", "x", "core")


EPS = 1e-06
THETA = 1000000.0


def rms_scale(values, gain):
    wide = values.astype(jnp.float32)
    spread = jnp.mean(wide * wide, axis=-1, keepdims=True)
    return (wide * lax.rsqrt(spread + EPS) * gain.astype(jnp.float32)).astype(jnp.bfloat16)


def rotate(vectors, positions):
    middle = vectors.shape[-1] // 2
    frequency = THETA ** (-(jnp.arange(middle, dtype=jnp.float32) * 2.0 / vectors.shape[-1]))
    angles = positions.astype(jnp.float32)[:, None] * frequency[None, :]
    angles = jnp.concatenate([angles, angles], axis=-1)[:, None, :]
    turned = jnp.concatenate([-vectors[..., middle:], vectors[..., :middle]], axis=-1)
    return vectors * jnp.cos(angles) + turned * jnp.sin(angles)


def attend(queries, keys_all, values_all, context, span_len):
    row_count = queries.shape[0]
    head_count = queries.shape[1]
    head_size = queries.shape[2]
    block_rows = math.gcd(row_count, 512)
    block_count = row_count // block_rows
    scale = 1.0 / math.sqrt(head_size)
    key_pos = jnp.arange(keys_all.shape[0], dtype=jnp.int32)

    def one_block(items):
        query_block, start = items
        scores = (
            jnp.einsum("qhd,khd->hqk", query_block, keys_all, preferred_element_type=jnp.float32)
            * scale
        )
        query_pos = start + jnp.arange(block_rows, dtype=jnp.int32)
        allowed = jnp.where(
            key_pos[None, :] < span_len,
            key_pos[None, :] < context,
            key_pos[None, :] - span_len <= query_pos[:, None],
        )
        scores = jnp.where(allowed[None], scores, -1e30)
        largest = jnp.max(scores, axis=-1, keepdims=True)
        weights = jnp.where(allowed[None], jnp.exp(scores - largest), 0.0)
        probs = (weights / jnp.sum(weights, axis=-1, keepdims=True)).astype(jnp.bfloat16)
        return jnp.einsum(
            "hqk,khd->qhd", probs, values_all, preferred_element_type=jnp.float32
        ).astype(jnp.bfloat16)

    starts = jnp.arange(block_count, dtype=jnp.int32) * block_rows
    result = lax.map(
        one_block, (queries.reshape(block_count, block_rows, head_count, head_size), starts)
    )
    return result.reshape(row_count, head_count, head_size)


def per_device(
    hidden_in,
    context_len,
    page_table,
    paged_cache,
    attn_gain,
    proj_weight,
    proj_bias,
    out_weight,
    mlp_gain,
    expert_ids,
    route_weight,
    w_experts_in,
    w_experts_out,
    w_shared_in,
    w_shared_out,
    shared_gate,
):
    tok_rows = hidden_in.shape[0]
    width = hidden_in.shape[1]
    head_lanes = lax.axis_size(HEAD)
    device_count = lax.axis_size("tok") * head_lanes
    expert_count = device_count // 2
    top_count = expert_ids.shape[1]
    capacity = 2 * max(1, tok_rows * top_count * 5 // (8 * expert_count))
    gathered = lax.all_gather(hidden_in, HEAD, axis=0, tiled=True)
    stretch_rows = gathered.shape[0]
    heads_here = proj_weight.shape[2] // HD
    normed = rms_scale(gathered, attn_gain)
    projected = (
        jnp.einsum("td,cdf->ctf", normed, proj_weight, preferred_element_type=jnp.float32)
        + proj_bias.astype(jnp.float32)[:, None, :]
    )
    context = context_len[0]
    positions = context + jnp.arange(stretch_rows, dtype=jnp.int32)
    queries = rotate(projected[0].reshape(stretch_rows, heads_here, HD), positions).astype(
        jnp.bfloat16
    )
    new_keys = rotate(projected[1].reshape(stretch_rows, heads_here, HD), positions).astype(
        jnp.bfloat16
    )
    new_values = projected[2].reshape(stretch_rows, heads_here, HD).astype(jnp.bfloat16)
    ordered = jnp.take(paged_cache, page_table[0], axis=1)
    span_len = ordered.shape[1] * ordered.shape[2]
    ordered = ordered.reshape(2, span_len, heads_here, HD)
    keys_all = jnp.concatenate([ordered[0], new_keys], axis=0)
    values_all = jnp.concatenate([ordered[1], new_values], axis=0)
    heads_out = attend(queries, keys_all, values_all, context, span_len).reshape(
        stretch_rows, heads_here * HD
    )
    attn_own = lax.psum_scatter(
        jnp.dot(heads_out, out_weight, preferred_element_type=jnp.float32).astype(jnp.bfloat16),
        HEAD,
        scatter_dimension=0,
        tiled=True,
    ).astype(jnp.float32)
    resid = (hidden_in.astype(jnp.float32) + attn_own).astype(jnp.bfloat16)
    mixed = rms_scale(resid, mlp_gain)
    inner = jnp.einsum(
        "td,dcf->tcf",
        lax.all_gather(mixed, HEAD, axis=0, tiled=True),
        w_shared_in,
        preferred_element_type=jnp.float32,
    )
    activated = (jax.nn.silu(inner[:, 0]) * inner[:, 1]).astype(jnp.bfloat16)
    shared_part = jnp.dot(activated, w_shared_out, preferred_element_type=jnp.float32)
    shared_own = lax.psum_scatter(
        shared_part.astype(jnp.bfloat16), HEAD, scatter_dimension=0, tiled=True
    ).astype(jnp.float32)
    gate = jax.nn.sigmoid(jnp.dot(mixed, shared_gate, preferred_element_type=jnp.float32))
    flat_ids = expert_ids.reshape(-1)
    one_hot = (flat_ids[:, None] == jnp.arange(expert_count, dtype=jnp.int32)[None, :]).astype(
        jnp.int32
    )
    earlier = jnp.cumsum(one_hot, axis=0) - one_hot
    slot_pos = jnp.sum(earlier * one_hot, axis=1)
    slot_index = flat_ids * capacity + slot_pos
    slot_table = slot_index.reshape(tok_rows, top_count)
    dispatch_matrix = jnp.sum(
        (
            jnp.arange(expert_count * capacity, dtype=jnp.int32)[:, None, None] == slot_table[None]
        ).astype(jnp.int32),
        axis=2,
    ).astype(jnp.bfloat16)
    buffer = jnp.dot(dispatch_matrix, mixed, preferred_element_type=jnp.float32).astype(
        jnp.bfloat16
    )
    pair = [(0, 1), (1, 0)]
    arrived = lax.all_to_all(
        buffer.reshape(expert_count, capacity, width), ("tok", "x"), 0, 0, tiled=True
    ).reshape(expert_count * capacity, width)
    sibling = lax.ppermute(arrived, "core", pair)

    def half_expert(rows):
        inner = jnp.dot(rows, w_experts_in[0], preferred_element_type=jnp.float32)
        middle = inner.shape[1] // 2
        activated = (jax.nn.silu(inner[:, :middle]) * inner[:, middle:]).astype(jnp.bfloat16)
        return jnp.dot(activated, w_experts_out[0], preferred_element_type=jnp.float32).astype(
            jnp.bfloat16
        )

    part_own = half_expert(arrived)
    part_back = lax.ppermute(half_expert(sibling), "core", pair)
    merged_own = (part_own.astype(jnp.float32) + part_back.astype(jnp.float32)).astype(
        jnp.bfloat16
    )
    merged = lax.all_to_all(
        merged_own.reshape(expert_count, capacity, width), ("tok", "x"), 0, 0, tiled=True
    )
    picked = jnp.take(merged.reshape(expert_count * capacity, width), slot_index, axis=0).reshape(
        tok_rows, top_count, width
    )
    routed = jnp.sum(route_weight[:, :, None] * picked.astype(jnp.float32), axis=1)
    return (resid.astype(jnp.float32) + gate[:, None] * shared_own + routed).astype(jnp.bfloat16)


def solution(mesh):
    split = Mesh(
        mesh.devices.reshape(mesh.shape["tok"], mesh.shape["head"] // 2, 2), ("tok", "x", "core")
    )
    in_specs = (
        P(ROWS, None),
        P("tok"),
        P("tok", None),
        P(None, "tok", None, HEAD),
        P(),
        P(None, None, HEAD),
        P(None, HEAD),
        P(HEAD, None),
        P(),
        P(ROWS, None),
        P(ROWS, None),
        P(ROWS, None, None),
        P(ROWS, None, None),
        P(None, None, HEAD),
        P(HEAD, None),
        P(),
    )
    out_specs = P(ROWS, None)
    return jax.shard_map(
        per_device, mesh=split, in_specs=in_specs, out_specs=out_specs, check_vma=False
    )
```

```python
import math

import jax
import jax.numpy as jnp
from jax import lax
from jax.experimental import pallas as pl
from jax.experimental.pallas import tpu as pltpu
from jax.sharding import Mesh, PartitionSpec as P

HD = 128
HEAD = ("x", "core")
ROWS = ("tok", "x", "core")


EPS = 1e-06
THETA = 1000000.0


def rms_scale(values, gain):
    wide = values.astype(jnp.float32)
    spread = jnp.mean(wide * wide, axis=-1, keepdims=True)
    return (wide * lax.rsqrt(spread + EPS) * gain.astype(jnp.float32)).astype(jnp.bfloat16)


def rotate(vectors, positions):
    middle = vectors.shape[-1] // 2
    frequency = THETA ** (-(jnp.arange(middle, dtype=jnp.float32) * 2.0 / vectors.shape[-1]))
    angles = positions.astype(jnp.float32)[:, None] * frequency[None, :]
    angles = jnp.concatenate([angles, angles], axis=-1)[:, None, :]
    turned = jnp.concatenate([-vectors[..., middle:], vectors[..., :middle]], axis=-1)
    return vectors * jnp.cos(angles) + turned * jnp.sin(angles)


def attend(queries, keys_all, values_all, context, span_len):
    row_count = queries.shape[0]
    head_count = queries.shape[1]
    head_size = queries.shape[2]
    key_count = keys_all.shape[0]
    block_rows = math.gcd(row_count, 256)
    scale = 1.0 / math.sqrt(head_size)

    def kernel(context_ref, query_ref, key_ref, value_ref, out_ref):
        scores = (
            lax.dot_general(
                query_ref[...],
                key_ref[...],
                (((1,), (1,)), ((), ())),
                preferred_element_type=jnp.float32,
            )
            * scale
        )
        key_pos = lax.broadcasted_iota(jnp.int32, scores.shape, 1)
        query_pos = pl.program_id(1) * block_rows + lax.broadcasted_iota(
            jnp.int32, scores.shape, 0
        )
        cached = key_pos < span_len
        allowed = (cached & (key_pos < context_ref[0])) | (
            jnp.logical_not(cached) & (key_pos - span_len <= query_pos)
        )
        scores = jnp.where(allowed, scores, -1e30)
        largest = jnp.max(scores, axis=-1, keepdims=True)
        weights = jnp.where(allowed, jnp.exp(scores - largest), 0.0)
        probs = (weights / jnp.sum(weights, axis=-1, keepdims=True)).astype(jnp.bfloat16)
        out_ref[...] = jnp.dot(probs, value_ref[...], preferred_element_type=jnp.float32).astype(
            jnp.bfloat16
        )

    width = head_count * head_size
    result = pl.pallas_call(
        kernel,
        out_shape=jax.ShapeDtypeStruct((row_count, width), jnp.bfloat16),
        grid_spec=pltpu.PrefetchScalarGridSpec(
            num_scalar_prefetch=1,
            grid=(head_count, row_count // block_rows),
            in_specs=[
                pl.BlockSpec((block_rows, head_size), lambda h, i, c: (i, h)),
                pl.BlockSpec((key_count, head_size), lambda h, i, c: (0, h)),
                pl.BlockSpec((key_count, head_size), lambda h, i, c: (0, h)),
            ],
            out_specs=pl.BlockSpec((block_rows, head_size), lambda h, i, c: (i, h)),
        ),
    )(
        jnp.reshape(context, (1,)).astype(jnp.int32),
        queries.reshape(row_count, width),
        keys_all.reshape(key_count, width),
        values_all.reshape(key_count, width),
    )
    return result


def per_device(
    hidden_in,
    context_len,
    page_table,
    paged_cache,
    attn_gain,
    proj_weight,
    proj_bias,
    out_weight,
    mlp_gain,
    expert_ids,
    route_weight,
    w_experts_in,
    w_experts_out,
    w_shared_in,
    w_shared_out,
    shared_gate,
):
    tok_rows = hidden_in.shape[0]
    width = hidden_in.shape[1]
    head_lanes = lax.axis_size(HEAD)
    device_count = lax.axis_size("tok") * head_lanes
    expert_count = device_count // 2
    top_count = expert_ids.shape[1]
    capacity = 2 * max(1, tok_rows * top_count * 5 // (8 * expert_count))
    gathered = lax.all_gather(hidden_in, HEAD, axis=0, tiled=True)
    stretch_rows = gathered.shape[0]
    heads_here = proj_weight.shape[2] // HD
    normed = rms_scale(gathered, attn_gain)
    projected = (
        jnp.einsum("td,cdf->ctf", normed, proj_weight, preferred_element_type=jnp.float32)
        + proj_bias.astype(jnp.float32)[:, None, :]
    )
    context = context_len[0]
    positions = context + jnp.arange(stretch_rows, dtype=jnp.int32)
    queries = rotate(projected[0].reshape(stretch_rows, heads_here, HD), positions).astype(
        jnp.bfloat16
    )
    new_keys = rotate(projected[1].reshape(stretch_rows, heads_here, HD), positions).astype(
        jnp.bfloat16
    )
    new_values = projected[2].reshape(stretch_rows, heads_here, HD).astype(jnp.bfloat16)
    ordered = jnp.take(paged_cache, page_table[0], axis=1)
    span_len = ordered.shape[1] * ordered.shape[2]
    ordered = ordered.reshape(2, span_len, heads_here, HD)
    keys_all = jnp.concatenate([ordered[0], new_keys], axis=0)
    values_all = jnp.concatenate([ordered[1], new_values], axis=0)
    heads_out = attend(queries, keys_all, values_all, context, span_len).reshape(
        stretch_rows, heads_here * HD
    )
    attn_own = lax.psum_scatter(
        jnp.dot(heads_out, out_weight, preferred_element_type=jnp.float32).astype(jnp.bfloat16),
        HEAD,
        scatter_dimension=0,
        tiled=True,
    ).astype(jnp.float32)
    resid = (hidden_in.astype(jnp.float32) + attn_own).astype(jnp.bfloat16)
    mixed = rms_scale(resid, mlp_gain)
    inner = jnp.einsum(
        "td,dcf->tcf",
        lax.all_gather(mixed, HEAD, axis=0, tiled=True),
        w_shared_in,
        preferred_element_type=jnp.float32,
    )
    activated = (jax.nn.silu(inner[:, 0]) * inner[:, 1]).astype(jnp.bfloat16)
    shared_part = jnp.dot(activated, w_shared_out, preferred_element_type=jnp.float32)
    shared_own = lax.psum_scatter(
        shared_part.astype(jnp.bfloat16), HEAD, scatter_dimension=0, tiled=True
    ).astype(jnp.float32)
    gate = jax.nn.sigmoid(jnp.dot(mixed, shared_gate, preferred_element_type=jnp.float32))
    flat_ids = expert_ids.reshape(-1)
    one_hot = (flat_ids[:, None] == jnp.arange(expert_count, dtype=jnp.int32)[None, :]).astype(
        jnp.int32
    )
    earlier = jnp.cumsum(one_hot, axis=0) - one_hot
    slot_pos = jnp.sum(earlier * one_hot, axis=1)
    slot_index = flat_ids * capacity + slot_pos
    slot_table = slot_index.reshape(tok_rows, top_count)
    dispatch_matrix = jnp.sum(
        (
            jnp.arange(expert_count * capacity, dtype=jnp.int32)[:, None, None] == slot_table[None]
        ).astype(jnp.int32),
        axis=2,
    ).astype(jnp.bfloat16)
    buffer = jnp.dot(dispatch_matrix, mixed, preferred_element_type=jnp.float32).astype(
        jnp.bfloat16
    )
    pair = [(0, 1), (1, 0)]
    arrived = lax.all_to_all(
        buffer.reshape(expert_count, capacity, width), ("tok", "x"), 0, 0, tiled=True
    ).reshape(expert_count * capacity, width)
    sibling = lax.ppermute(arrived, "core", pair)

    def half_expert(rows):
        inner = jnp.dot(rows, w_experts_in[0], preferred_element_type=jnp.float32)
        middle = inner.shape[1] // 2
        activated = (jax.nn.silu(inner[:, :middle]) * inner[:, middle:]).astype(jnp.bfloat16)
        return jnp.dot(activated, w_experts_out[0], preferred_element_type=jnp.float32).astype(
            jnp.bfloat16
        )

    part_own = half_expert(arrived)
    part_back = lax.ppermute(half_expert(sibling), "core", pair)
    merged_own = (part_own.astype(jnp.float32) + part_back.astype(jnp.float32)).astype(
        jnp.bfloat16
    )
    merged = lax.all_to_all(
        merged_own.reshape(expert_count, capacity, width), ("tok", "x"), 0, 0, tiled=True
    )
    picked = jnp.take(merged.reshape(expert_count * capacity, width), slot_index, axis=0).reshape(
        tok_rows, top_count, width
    )
    routed = jnp.sum(route_weight[:, :, None] * picked.astype(jnp.float32), axis=1)
    return (resid.astype(jnp.float32) + gate[:, None] * shared_own + routed).astype(jnp.bfloat16)


def solution(mesh):
    split = Mesh(
        mesh.devices.reshape(mesh.shape["tok"], mesh.shape["head"] // 2, 2), ("tok", "x", "core")
    )
    in_specs = (
        P(ROWS, None),
        P("tok"),
        P("tok", None),
        P(None, "tok", None, HEAD),
        P(),
        P(None, None, HEAD),
        P(None, HEAD),
        P(HEAD, None),
        P(),
        P(ROWS, None),
        P(ROWS, None),
        P(ROWS, None, None),
        P(ROWS, None, None),
        P(None, None, HEAD),
        P(HEAD, None),
        P(),
    )
    out_specs = P(ROWS, None)
    return jax.shard_map(
        per_device, mesh=split, in_specs=in_specs, out_specs=out_specs, check_vma=False
    )
```

```python
import math

import jax
import jax.numpy as jnp
from jax import lax
from jax.experimental import pallas as pl
from jax.experimental.pallas import tpu as pltpu
from jax.sharding import Mesh, PartitionSpec as P

HD = 128
HEAD = ("x", "core")
ROWS = ("tok", "x", "core")


EPS = 1e-06
THETA = 1000000.0


def rms_scale(values, gain):
    wide = values.astype(jnp.float32)
    spread = jnp.mean(wide * wide, axis=-1, keepdims=True)
    return (wide * lax.rsqrt(spread + EPS) * gain.astype(jnp.float32)).astype(jnp.bfloat16)


def rotate(vectors, positions):
    middle = vectors.shape[-1] // 2
    frequency = THETA ** (-(jnp.arange(middle, dtype=jnp.float32) * 2.0 / vectors.shape[-1]))
    angles = positions.astype(jnp.float32)[:, None] * frequency[None, :]
    angles = jnp.concatenate([angles, angles], axis=-1)[:, None, :]
    turned = jnp.concatenate([-vectors[..., middle:], vectors[..., :middle]], axis=-1)
    return vectors * jnp.cos(angles) + turned * jnp.sin(angles)


def attend(queries, keys_all, values_all, context, span_len):
    row_count = queries.shape[0]
    head_count = queries.shape[1]
    head_size = queries.shape[2]
    key_count = keys_all.shape[0]
    block_rows = math.gcd(row_count, 256)
    scale = 1.0 / math.sqrt(head_size)

    def kernel(context_ref, query_ref, key_ref, value_ref, out_ref):
        scores = (
            lax.dot_general(
                query_ref[...],
                key_ref[...],
                (((1,), (1,)), ((), ())),
                preferred_element_type=jnp.float32,
            )
            * scale
        )
        key_pos = lax.broadcasted_iota(jnp.int32, scores.shape, 1)
        query_pos = pl.program_id(1) * block_rows + lax.broadcasted_iota(
            jnp.int32, scores.shape, 0
        )
        cached = key_pos < span_len
        allowed = (cached & (key_pos < context_ref[0])) | (
            jnp.logical_not(cached) & (key_pos - span_len <= query_pos)
        )
        scores = jnp.where(allowed, scores, -1e30)
        largest = jnp.max(scores, axis=-1, keepdims=True)
        weights = jnp.where(allowed, jnp.exp(scores - largest), 0.0)
        probs = (weights / jnp.sum(weights, axis=-1, keepdims=True)).astype(jnp.bfloat16)
        out_ref[...] = jnp.dot(probs, value_ref[...], preferred_element_type=jnp.float32).astype(
            jnp.bfloat16
        )

    width = head_count * head_size
    result = pl.pallas_call(
        kernel,
        out_shape=jax.ShapeDtypeStruct((row_count, width), jnp.bfloat16),
        grid_spec=pltpu.PrefetchScalarGridSpec(
            num_scalar_prefetch=1,
            grid=(head_count, row_count // block_rows),
            in_specs=[
                pl.BlockSpec((block_rows, head_size), lambda h, i, c: (i, h)),
                pl.BlockSpec((key_count, head_size), lambda h, i, c: (0, h)),
                pl.BlockSpec((key_count, head_size), lambda h, i, c: (0, h)),
            ],
            out_specs=pl.BlockSpec((block_rows, head_size), lambda h, i, c: (i, h)),
        ),
    )(
        jnp.reshape(context, (1,)).astype(jnp.int32),
        queries.reshape(row_count, width),
        keys_all.reshape(key_count, width),
        values_all.reshape(key_count, width),
    )
    return result


def per_device(
    hidden_in,
    context_len,
    page_table,
    paged_cache,
    attn_gain,
    proj_weight,
    proj_bias,
    out_weight,
    mlp_gain,
    expert_ids,
    route_weight,
    w_experts_in,
    w_experts_out,
    w_shared_in,
    w_shared_out,
    shared_gate,
):
    tok_rows = hidden_in.shape[0]
    width = hidden_in.shape[1]
    head_lanes = lax.axis_size(HEAD)
    device_count = lax.axis_size("tok") * head_lanes
    expert_count = device_count // 2
    top_count = expert_ids.shape[1]
    capacity = 2 * max(1, tok_rows * top_count * 5 // (8 * expert_count))
    gathered = lax.all_gather(hidden_in, HEAD, axis=0, tiled=True)
    stretch_rows = gathered.shape[0]
    heads_here = proj_weight.shape[2] // HD
    normed = rms_scale(gathered, attn_gain)
    projected = (
        jnp.einsum("td,cdf->ctf", normed, proj_weight, preferred_element_type=jnp.float32)
        + proj_bias.astype(jnp.float32)[:, None, :]
    )
    context = context_len[0]
    positions = context + jnp.arange(stretch_rows, dtype=jnp.int32)
    queries = rotate(projected[0].reshape(stretch_rows, heads_here, HD), positions).astype(
        jnp.bfloat16
    )
    new_keys = rotate(projected[1].reshape(stretch_rows, heads_here, HD), positions).astype(
        jnp.bfloat16
    )
    new_values = projected[2].reshape(stretch_rows, heads_here, HD).astype(jnp.bfloat16)
    ordered = jnp.take(paged_cache, page_table[0], axis=1)
    span_len = ordered.shape[1] * ordered.shape[2]
    ordered = ordered.reshape(2, span_len, heads_here, HD)
    keys_all = jnp.concatenate([ordered[0], new_keys], axis=0)
    values_all = jnp.concatenate([ordered[1], new_values], axis=0)
    heads_out = attend(queries, keys_all, values_all, context, span_len).reshape(
        stretch_rows, heads_here * HD
    )
    attn_own = lax.psum_scatter(
        jnp.dot(heads_out, out_weight, preferred_element_type=jnp.float32).astype(jnp.bfloat16),
        HEAD,
        scatter_dimension=0,
        tiled=True,
    ).astype(jnp.float32)
    resid = (hidden_in.astype(jnp.float32) + attn_own).astype(jnp.bfloat16)
    mixed = rms_scale(resid, mlp_gain)
    inner = jnp.einsum(
        "td,dcf->tcf",
        lax.all_gather(mixed, HEAD, axis=0, tiled=True),
        w_shared_in,
        preferred_element_type=jnp.float32,
    )
    activated = (jax.nn.silu(inner[:, 0]) * inner[:, 1]).astype(jnp.bfloat16)
    shared_part = jnp.dot(activated, w_shared_out, preferred_element_type=jnp.float32)
    shared_own = lax.psum_scatter(
        shared_part.astype(jnp.bfloat16), HEAD, scatter_dimension=0, tiled=True
    ).astype(jnp.float32)
    gate = jax.nn.sigmoid(jnp.dot(mixed, shared_gate, preferred_element_type=jnp.float32))
    flat_ids = expert_ids.reshape(-1)
    one_hot = (flat_ids[:, None] == jnp.arange(expert_count, dtype=jnp.int32)[None, :]).astype(
        jnp.int32
    )
    earlier = jnp.cumsum(one_hot, axis=0) - one_hot
    slot_pos = jnp.sum(earlier * one_hot, axis=1)
    slot_index = flat_ids * capacity + slot_pos
    slot_table = slot_index.reshape(tok_rows, top_count)
    dispatch_matrix = jnp.sum(
        (
            jnp.arange(expert_count * capacity, dtype=jnp.int32)[:, None, None] == slot_table[None]
        ).astype(jnp.int32),
        axis=2,
    ).astype(jnp.bfloat16)
    buffer = jnp.dot(dispatch_matrix, mixed, preferred_element_type=jnp.float32).astype(
        jnp.bfloat16
    )
    pair = [(0, 1), (1, 0)]
    arrived = lax.all_to_all(buffer, ("tok", "x"), 0, 0, tiled=True)
    sibling = lax.ppermute(arrived, "core", pair)

    def half_expert(rows):
        inner = jnp.dot(rows, w_experts_in[0], preferred_element_type=jnp.float32)
        middle = inner.shape[1] // 2
        activated = (jax.nn.silu(inner[:, :middle]) * inner[:, middle:]).astype(jnp.bfloat16)
        return jnp.dot(activated, w_experts_out[0], preferred_element_type=jnp.float32).astype(
            jnp.bfloat16
        )

    part_own = half_expert(arrived)
    part_back = lax.ppermute(half_expert(sibling), "core", pair)
    merged_own = (part_own.astype(jnp.float32) + part_back.astype(jnp.float32)).astype(
        jnp.bfloat16
    )
    merged = lax.all_to_all(merged_own, ("tok", "x"), 0, 0, tiled=True)
    combine = jnp.sum(
        jnp.where(
            jnp.arange(expert_count * capacity, dtype=jnp.int32)[None, None, :]
            == slot_table[:, :, None],
            route_weight[:, :, None],
            0.0,
        ),
        axis=1,
    )
    routed = jnp.dot(
        combine,
        merged.astype(jnp.float32),
        precision=lax.Precision.HIGHEST,
        preferred_element_type=jnp.float32,
    )
    return (resid.astype(jnp.float32) + gate[:, None] * shared_own + routed).astype(jnp.bfloat16)


def solution(mesh):
    split = Mesh(
        mesh.devices.reshape(mesh.shape["tok"], mesh.shape["head"] // 2, 2), ("tok", "x", "core")
    )
    in_specs = (
        P(ROWS, None),
        P("tok"),
        P("tok", None),
        P(None, "tok", None, HEAD),
        P(),
        P(None, None, HEAD),
        P(None, HEAD),
        P(HEAD, None),
        P(),
        P(ROWS, None),
        P(ROWS, None),
        P(ROWS, None, None),
        P(ROWS, None, None),
        P(None, None, HEAD),
        P(HEAD, None),
        P(),
    )
    out_specs = P(ROWS, None)
    return jax.shard_map(
        per_device, mesh=split, in_specs=in_specs, out_specs=out_specs, check_vma=False
    )
```

```python
import math

import jax
import jax.numpy as jnp
from jax import lax
from jax.experimental import pallas as pl
from jax.experimental.pallas import tpu as pltpu
from jax.sharding import Mesh, PartitionSpec as P

HD = 128
HEAD = ("x", "core")
ROWS = ("tok", "x", "core")


EPS = 1e-06
THETA = 1000000.0


def rms_scale(values, gain):
    wide = values.astype(jnp.float32)
    spread = jnp.mean(wide * wide, axis=-1, keepdims=True)
    return (wide * lax.rsqrt(spread + EPS) * gain.astype(jnp.float32)).astype(jnp.bfloat16)


def rotate(vectors, positions):
    middle = vectors.shape[-1] // 2
    frequency = THETA ** (-(jnp.arange(middle, dtype=jnp.float32) * 2.0 / vectors.shape[-1]))
    angles = positions.astype(jnp.float32)[:, None] * frequency[None, :]
    angles = jnp.concatenate([angles, angles], axis=-1)[:, None, :]
    turned = jnp.concatenate([-vectors[..., middle:], vectors[..., :middle]], axis=-1)
    return vectors * jnp.cos(angles) + turned * jnp.sin(angles)


def attend(queries, keys_all, values_all, context, span_len):
    row_count = queries.shape[0]
    head_count = queries.shape[1]
    head_size = queries.shape[2]
    key_count = keys_all.shape[0]
    block_rows = math.gcd(row_count, 256)
    scale = 1.0 / math.sqrt(head_size)

    def kernel(context_ref, query_ref, key_ref, value_ref, out_ref):
        scores = (
            lax.dot_general(
                query_ref[...],
                key_ref[...],
                (((1,), (1,)), ((), ())),
                preferred_element_type=jnp.float32,
            )
            * scale
        )
        key_pos = lax.broadcasted_iota(jnp.int32, scores.shape, 1)
        query_pos = pl.program_id(1) * block_rows + lax.broadcasted_iota(
            jnp.int32, scores.shape, 0
        )
        cached = key_pos < span_len
        allowed = (cached & (key_pos < context_ref[0])) | (
            jnp.logical_not(cached) & (key_pos - span_len <= query_pos)
        )
        scores = jnp.where(allowed, scores, -1e30)
        largest = jnp.max(scores, axis=-1, keepdims=True)
        weights = jnp.where(allowed, jnp.exp(scores - largest), 0.0)
        probs = (weights / jnp.sum(weights, axis=-1, keepdims=True)).astype(jnp.bfloat16)
        out_ref[...] = jnp.dot(probs, value_ref[...], preferred_element_type=jnp.float32).astype(
            jnp.bfloat16
        )

    width = head_count * head_size
    result = pl.pallas_call(
        kernel,
        out_shape=jax.ShapeDtypeStruct((row_count, width), jnp.bfloat16),
        grid_spec=pltpu.PrefetchScalarGridSpec(
            num_scalar_prefetch=1,
            grid=(head_count, row_count // block_rows),
            in_specs=[
                pl.BlockSpec((block_rows, head_size), lambda h, i, c: (i, h)),
                pl.BlockSpec((key_count, head_size), lambda h, i, c: (0, h)),
                pl.BlockSpec((key_count, head_size), lambda h, i, c: (0, h)),
            ],
            out_specs=pl.BlockSpec((block_rows, head_size), lambda h, i, c: (i, h)),
        ),
    )(
        jnp.reshape(context, (1,)).astype(jnp.int32),
        queries.reshape(row_count, width),
        keys_all.reshape(key_count, width),
        values_all.reshape(key_count, width),
    )
    return result


def per_device(
    hidden_in,
    context_len,
    page_table,
    paged_cache,
    attn_gain,
    proj_weight,
    proj_bias,
    out_weight,
    mlp_gain,
    expert_ids,
    route_weight,
    w_experts_in,
    w_experts_out,
    w_shared_in,
    w_shared_out,
    shared_gate,
):
    tok_rows = hidden_in.shape[0]
    width = hidden_in.shape[1]
    head_lanes = lax.axis_size(HEAD)
    device_count = lax.axis_size("tok") * head_lanes
    expert_count = device_count // 2
    top_count = expert_ids.shape[1]
    capacity = 2 * max(1, tok_rows * top_count * 5 // (8 * expert_count))
    gathered = lax.all_gather(hidden_in, HEAD, axis=0, tiled=True)
    stretch_rows = gathered.shape[0]
    heads_here = proj_weight.shape[2] // HD
    normed = rms_scale(gathered, attn_gain)
    projected = (
        jnp.einsum("td,cdf->ctf", normed, proj_weight, preferred_element_type=jnp.float32)
        + proj_bias.astype(jnp.float32)[:, None, :]
    )
    context = context_len[0]
    positions = context + jnp.arange(stretch_rows, dtype=jnp.int32)
    queries = rotate(projected[0].reshape(stretch_rows, heads_here, HD), positions).astype(
        jnp.bfloat16
    )
    new_keys = rotate(projected[1].reshape(stretch_rows, heads_here, HD), positions).astype(
        jnp.bfloat16
    )
    new_values = projected[2].reshape(stretch_rows, heads_here, HD).astype(jnp.bfloat16)
    ordered = jnp.take(paged_cache, page_table[0], axis=1)
    span_len = ordered.shape[1] * ordered.shape[2]
    ordered = ordered.reshape(2, span_len, heads_here, HD)
    keys_all = jnp.concatenate([ordered[0], new_keys], axis=0)
    values_all = jnp.concatenate([ordered[1], new_values], axis=0)
    heads_out = attend(queries, keys_all, values_all, context, span_len).reshape(
        stretch_rows, heads_here * HD
    )
    attn_own = lax.psum_scatter(
        jnp.dot(heads_out, out_weight, preferred_element_type=jnp.float32).astype(jnp.bfloat16),
        HEAD,
        scatter_dimension=0,
        tiled=True,
    ).astype(jnp.float32)
    resid = (hidden_in.astype(jnp.float32) + attn_own).astype(jnp.bfloat16)
    mixed = rms_scale(resid, mlp_gain)
    inner = jnp.einsum(
        "td,dcf->tcf",
        lax.all_gather(mixed, HEAD, axis=0, tiled=True),
        w_shared_in,
        preferred_element_type=jnp.float32,
    )
    activated = (jax.nn.silu(inner[:, 0]) * inner[:, 1]).astype(jnp.bfloat16)
    shared_part = jnp.dot(activated, w_shared_out, preferred_element_type=jnp.float32)
    shared_own = lax.psum_scatter(
        shared_part.astype(jnp.bfloat16), HEAD, scatter_dimension=0, tiled=True
    ).astype(jnp.float32)
    gate = jax.nn.sigmoid(jnp.dot(mixed, shared_gate, preferred_element_type=jnp.float32))
    flat_ids = expert_ids.reshape(-1)
    one_hot = (flat_ids[:, None] == jnp.arange(expert_count, dtype=jnp.int32)[None, :]).astype(
        jnp.int32
    )
    earlier = jnp.cumsum(one_hot, axis=0) - one_hot
    slot_pos = jnp.sum(earlier * one_hot, axis=1)
    slot_index = flat_ids * capacity + slot_pos
    slot_table = slot_index.reshape(tok_rows, top_count)
    dispatch_matrix = jnp.sum(
        (
            jnp.arange(expert_count * capacity, dtype=jnp.int32)[:, None, None] == slot_table[None]
        ).astype(jnp.int32),
        axis=2,
    ).astype(jnp.bfloat16)
    buffer = jnp.dot(dispatch_matrix, mixed, preferred_element_type=jnp.float32).astype(
        jnp.bfloat16
    )
    pair = [(0, 1), (1, 0)]
    tiles = (expert_count, capacity, width // 128, 128)
    arrived = lax.all_to_all(buffer.reshape(tiles), ("tok", "x"), 0, 0, tiled=True).reshape(
        expert_count * capacity, width
    )
    sibling = lax.ppermute(arrived, "core", pair)

    def half_expert(rows):
        inner = jnp.dot(rows, w_experts_in[0], preferred_element_type=jnp.float32)
        middle = inner.shape[1] // 2
        activated = (jax.nn.silu(inner[:, :middle]) * inner[:, middle:]).astype(jnp.bfloat16)
        return jnp.dot(activated, w_experts_out[0], preferred_element_type=jnp.float32).astype(
            jnp.bfloat16
        )

    part_own = half_expert(arrived)
    part_back = lax.ppermute(half_expert(sibling), "core", pair)
    merged_own = (part_own.astype(jnp.float32) + part_back.astype(jnp.float32)).astype(
        jnp.bfloat16
    )
    merged = lax.all_to_all(merged_own.reshape(tiles), ("tok", "x"), 0, 0, tiled=True).reshape(
        expert_count * capacity, width
    )
    combine = jnp.sum(
        jnp.where(
            jnp.arange(expert_count * capacity, dtype=jnp.int32)[None, None, :]
            == slot_table[:, :, None],
            route_weight[:, :, None],
            0.0,
        ),
        axis=1,
    )
    routed = jnp.dot(
        combine,
        merged.astype(jnp.float32),
        precision=lax.Precision.HIGHEST,
        preferred_element_type=jnp.float32,
    )
    return (resid.astype(jnp.float32) + gate[:, None] * shared_own + routed).astype(jnp.bfloat16)


def solution(mesh):
    split = Mesh(
        mesh.devices.reshape(mesh.shape["tok"], mesh.shape["head"] // 2, 2), ("tok", "x", "core")
    )
    in_specs = (
        P(ROWS, None),
        P("tok"),
        P("tok", None),
        P(None, "tok", None, HEAD),
        P(),
        P(None, None, HEAD),
        P(None, HEAD),
        P(HEAD, None),
        P(),
        P(ROWS, None),
        P(ROWS, None),
        P(ROWS, None, None),
        P(ROWS, None, None),
        P(None, None, HEAD),
        P(HEAD, None),
        P(),
    )
    out_specs = P(ROWS, None)
    return jax.shard_map(
        per_device, mesh=split, in_specs=in_specs, out_specs=out_specs, check_vma=False
    )
```

```python
import math

import jax
import jax.numpy as jnp
from jax import lax
from jax.experimental import pallas as pl
from jax.experimental.pallas import tpu as pltpu
from jax.sharding import Mesh, PartitionSpec as P

HD = 128
HEAD = ("x", "core")
ROWS = ("tok", "x", "core")


EPS = 1e-06
THETA = 1000000.0


def rms_scale(values, gain):
    wide = values.astype(jnp.float32)
    spread = jnp.mean(wide * wide, axis=-1, keepdims=True)
    return (wide * lax.rsqrt(spread + EPS) * gain.astype(jnp.float32)).astype(jnp.bfloat16)


def rotate(vectors, positions):
    middle = vectors.shape[-1] // 2
    frequency = THETA ** (-(jnp.arange(middle, dtype=jnp.float32) * 2.0 / vectors.shape[-1]))
    angles = positions.astype(jnp.float32)[:, None] * frequency[None, :]
    angles = jnp.concatenate([angles, angles], axis=-1)[:, None, :]
    turned = jnp.concatenate([-vectors[..., middle:], vectors[..., :middle]], axis=-1)
    return vectors * jnp.cos(angles) + turned * jnp.sin(angles)


def attend(queries, keys_all, values_all, context, span_len):
    row_count = queries.shape[0]
    head_count = queries.shape[1]
    head_size = queries.shape[2]
    key_count = keys_all.shape[0]
    block_rows = math.gcd(row_count, 256)
    scale = 1.0 / math.sqrt(head_size)

    def kernel(context_ref, query_ref, key_ref, value_ref, out_ref):
        scores = (
            lax.dot_general(
                query_ref[...],
                key_ref[...],
                (((1,), (1,)), ((), ())),
                preferred_element_type=jnp.float32,
            )
            * scale
        )
        key_pos = lax.broadcasted_iota(jnp.int32, scores.shape, 1)
        query_pos = pl.program_id(1) * block_rows + lax.broadcasted_iota(
            jnp.int32, scores.shape, 0
        )
        cached = key_pos < span_len
        allowed = (cached & (key_pos < context_ref[0])) | (
            jnp.logical_not(cached) & (key_pos - span_len <= query_pos)
        )
        scores = jnp.where(allowed, scores, -1e30)
        largest = jnp.max(scores, axis=-1, keepdims=True)
        weights = jnp.where(allowed, jnp.exp(scores - largest), 0.0)
        probs = (weights / jnp.sum(weights, axis=-1, keepdims=True)).astype(jnp.bfloat16)
        out_ref[...] = jnp.dot(probs, value_ref[...], preferred_element_type=jnp.float32).astype(
            jnp.bfloat16
        )

    width = head_count * head_size
    result = pl.pallas_call(
        kernel,
        out_shape=jax.ShapeDtypeStruct((row_count, width), jnp.bfloat16),
        grid_spec=pltpu.PrefetchScalarGridSpec(
            num_scalar_prefetch=1,
            grid=(head_count, row_count // block_rows),
            in_specs=[
                pl.BlockSpec((block_rows, head_size), lambda h, i, c: (i, h)),
                pl.BlockSpec((key_count, head_size), lambda h, i, c: (0, h)),
                pl.BlockSpec((key_count, head_size), lambda h, i, c: (0, h)),
            ],
            out_specs=pl.BlockSpec((block_rows, head_size), lambda h, i, c: (i, h)),
        ),
    )(
        jnp.reshape(context, (1,)).astype(jnp.int32),
        queries.reshape(row_count, width),
        keys_all.reshape(key_count, width),
        values_all.reshape(key_count, width),
    )
    return result


def per_device(
    hidden_in,
    context_len,
    page_table,
    paged_cache,
    attn_gain,
    proj_weight,
    proj_bias,
    out_weight,
    mlp_gain,
    expert_ids,
    route_weight,
    w_experts_in,
    w_experts_out,
    w_shared_in,
    w_shared_out,
    shared_gate,
):
    tok_rows = hidden_in.shape[0]
    width = hidden_in.shape[1]
    head_lanes = lax.axis_size(HEAD)
    device_count = lax.axis_size("tok") * head_lanes
    expert_count = device_count // 2
    top_count = expert_ids.shape[1]
    capacity = 2 * max(1, tok_rows * top_count * 5 // (8 * expert_count))
    gathered = lax.all_gather(hidden_in, HEAD, axis=0, tiled=True)
    stretch_rows = gathered.shape[0]
    heads_here = proj_weight.shape[2] // HD
    normed = rms_scale(gathered, attn_gain)
    projected = (
        jnp.einsum("td,cdf->ctf", normed, proj_weight, preferred_element_type=jnp.float32)
        + proj_bias.astype(jnp.float32)[:, None, :]
    )
    context = context_len[0]
    positions = context + jnp.arange(stretch_rows, dtype=jnp.int32)
    queries = rotate(projected[0].reshape(stretch_rows, heads_here, HD), positions).astype(
        jnp.bfloat16
    )
    new_keys = rotate(projected[1].reshape(stretch_rows, heads_here, HD), positions).astype(
        jnp.bfloat16
    )
    new_values = projected[2].reshape(stretch_rows, heads_here, HD).astype(jnp.bfloat16)
    ordered = jnp.take(paged_cache, page_table[0], axis=1)
    span_len = ordered.shape[1] * ordered.shape[2]
    ordered = ordered.reshape(2, span_len, heads_here, HD)
    keys_all = jnp.concatenate([ordered[0], new_keys], axis=0)
    values_all = jnp.concatenate([ordered[1], new_values], axis=0)
    heads_out = attend(queries, keys_all, values_all, context, span_len).reshape(
        stretch_rows, heads_here * HD
    )
    attn_own = lax.psum_scatter(
        jnp.dot(heads_out, out_weight, preferred_element_type=jnp.float32).astype(jnp.bfloat16),
        HEAD,
        scatter_dimension=0,
        tiled=True,
    ).astype(jnp.float32)
    resid = (hidden_in.astype(jnp.float32) + attn_own).astype(jnp.bfloat16)
    mixed = rms_scale(resid, mlp_gain)
    gate = jax.nn.sigmoid(jnp.dot(mixed, shared_gate, preferred_element_type=jnp.float32))
    flat_ids = expert_ids.reshape(-1)
    one_hot = (flat_ids[:, None] == jnp.arange(expert_count, dtype=jnp.int32)[None, :]).astype(
        jnp.int32
    )
    earlier = jnp.cumsum(one_hot, axis=0) - one_hot
    slot_pos = jnp.sum(earlier * one_hot, axis=1)
    slot_index = flat_ids * capacity + slot_pos
    slot_table = slot_index.reshape(tok_rows, top_count)
    dispatch_matrix = jnp.sum(
        (
            jnp.arange(expert_count * capacity, dtype=jnp.int32)[:, None, None] == slot_table[None]
        ).astype(jnp.int32),
        axis=2,
    ).astype(jnp.bfloat16)
    buffer = jnp.dot(dispatch_matrix, mixed, preferred_element_type=jnp.float32).astype(
        jnp.bfloat16
    )
    pair = [(0, 1), (1, 0)]
    tiles = (expert_count, capacity, width // 128, 128)
    arrived = lax.all_to_all(buffer.reshape(tiles), ("tok", "x"), 0, 0, tiled=True).reshape(
        expert_count * capacity, width
    )
    sibling = lax.ppermute(arrived, "core", pair)
    arrived, mixed_late = lax.optimization_barrier((arrived, mixed))
    mixed_all = lax.all_gather(mixed_late, HEAD, axis=0, tiled=True)

    def half_expert(rows):
        inner = jnp.dot(rows, w_experts_in[0], preferred_element_type=jnp.float32)
        middle = inner.shape[1] // 2
        activated = (jax.nn.silu(inner[:, :middle]) * inner[:, middle:]).astype(jnp.bfloat16)
        return jnp.dot(activated, w_experts_out[0], preferred_element_type=jnp.float32).astype(
            jnp.bfloat16
        )

    part_own = half_expert(arrived)
    part_back = lax.ppermute(half_expert(sibling), "core", pair)
    merged_own = (part_own.astype(jnp.float32) + part_back.astype(jnp.float32)).astype(
        jnp.bfloat16
    )
    _, mixed_all = lax.optimization_barrier((merged_own, mixed_all))
    inner = jnp.einsum(
        "td,dcf->tcf",
        mixed_all,
        w_shared_in,
        preferred_element_type=jnp.float32,
    )
    activated = (jax.nn.silu(inner[:, 0]) * inner[:, 1]).astype(jnp.bfloat16)
    shared_part = jnp.dot(activated, w_shared_out, preferred_element_type=jnp.float32)
    shared_own = lax.psum_scatter(
        shared_part.astype(jnp.bfloat16), HEAD, scatter_dimension=0, tiled=True
    ).astype(jnp.float32)
    merged = lax.all_to_all(merged_own.reshape(tiles), ("tok", "x"), 0, 0, tiled=True).reshape(
        expert_count * capacity, width
    )
    combine = jnp.sum(
        jnp.where(
            jnp.arange(expert_count * capacity, dtype=jnp.int32)[None, None, :]
            == slot_table[:, :, None],
            route_weight[:, :, None],
            0.0,
        ),
        axis=1,
    )
    routed = jnp.dot(
        combine,
        merged.astype(jnp.float32),
        precision=lax.Precision.HIGHEST,
        preferred_element_type=jnp.float32,
    )
    return (resid.astype(jnp.float32) + gate[:, None] * shared_own + routed).astype(jnp.bfloat16)


def solution(mesh):
    split = Mesh(
        mesh.devices.reshape(mesh.shape["tok"], mesh.shape["head"] // 2, 2), ("tok", "x", "core")
    )
    in_specs = (
        P(ROWS, None),
        P("tok"),
        P("tok", None),
        P(None, "tok", None, HEAD),
        P(),
        P(None, None, HEAD),
        P(None, HEAD),
        P(HEAD, None),
        P(),
        P(ROWS, None),
        P(ROWS, None),
        P(ROWS, None, None),
        P(ROWS, None, None),
        P(None, None, HEAD),
        P(HEAD, None),
        P(),
    )
    out_specs = P(ROWS, None)
    return jax.shard_map(
        per_device, mesh=split, in_specs=in_specs, out_specs=out_specs, check_vma=False
    )
```

```python
import math

import jax
import jax.numpy as jnp
from jax import lax
from jax.experimental import pallas as pl
from jax.experimental.pallas import tpu as pltpu
from jax.sharding import Mesh, PartitionSpec as P

HD = 128
HEAD = ("x", "core")
ROWS = ("tok", "x", "core")


EPS = 1e-06
THETA = 1000000.0


def rms_scale(values, gain):
    wide = values.astype(jnp.float32)
    spread = jnp.mean(wide * wide, axis=-1, keepdims=True)
    return (wide * lax.rsqrt(spread + EPS) * gain.astype(jnp.float32)).astype(jnp.bfloat16)


def rotate(vectors, positions):
    middle = vectors.shape[-1] // 2
    frequency = THETA ** (-(jnp.arange(middle, dtype=jnp.float32) * 2.0 / vectors.shape[-1]))
    angles = positions.astype(jnp.float32)[:, None] * frequency[None, :]
    angles = jnp.concatenate([angles, angles], axis=-1)[:, None, :]
    turned = jnp.concatenate([-vectors[..., middle:], vectors[..., :middle]], axis=-1)
    return vectors * jnp.cos(angles) + turned * jnp.sin(angles)


def attend(queries, keys_all, values_all, context, span_len, group, part):
    row_count = queries.shape[0]
    head_count = queries.shape[1]
    head_size = queries.shape[2]
    key_count = keys_all.shape[0]
    block_rows = math.gcd(row_count, 256)
    scale = 1.0 / math.sqrt(head_size)

    def kernel(context_ref, query_ref, key_ref, value_ref, out_ref):
        scores = (
            lax.dot_general(
                query_ref[...],
                key_ref[...],
                (((1,), (1,)), ((), ())),
                preferred_element_type=jnp.float32,
            )
            * scale
        )
        key_pos = lax.broadcasted_iota(jnp.int32, scores.shape, 1)
        row = pl.program_id(1) * block_rows + lax.broadcasted_iota(jnp.int32, scores.shape, 0)
        shift = part.bit_length() - 1
        query_pos = ((row >> shift) << (shift + 1)) + group * part + (row & (part - 1))
        cached = key_pos < span_len
        allowed = (cached & (key_pos < context_ref[0])) | (
            jnp.logical_not(cached) & (key_pos - span_len <= query_pos)
        )
        scores = jnp.where(allowed, scores, -1e30)
        largest = jnp.max(scores, axis=-1, keepdims=True)
        weights = jnp.where(allowed, jnp.exp(scores - largest), 0.0)
        probs = (weights / jnp.sum(weights, axis=-1, keepdims=True)).astype(jnp.bfloat16)
        out_ref[...] = jnp.dot(probs, value_ref[...], preferred_element_type=jnp.float32).astype(
            jnp.bfloat16
        )

    width = head_count * head_size
    result = pl.pallas_call(
        kernel,
        out_shape=jax.ShapeDtypeStruct((row_count, width), jnp.bfloat16),
        grid_spec=pltpu.PrefetchScalarGridSpec(
            num_scalar_prefetch=1,
            grid=(head_count, row_count // block_rows),
            in_specs=[
                pl.BlockSpec((block_rows, head_size), lambda h, i, c: (i, h)),
                pl.BlockSpec((key_count, head_size), lambda h, i, c: (0, h)),
                pl.BlockSpec((key_count, head_size), lambda h, i, c: (0, h)),
            ],
            out_specs=pl.BlockSpec((block_rows, head_size), lambda h, i, c: (i, h)),
        ),
    )(
        jnp.reshape(context, (1,)).astype(jnp.int32),
        queries.reshape(row_count, width),
        keys_all.reshape(key_count, width),
        values_all.reshape(key_count, width),
    )
    return result


def per_device(
    hidden_in,
    context_len,
    page_table,
    paged_cache,
    attn_gain,
    proj_weight,
    proj_bias,
    out_weight,
    mlp_gain,
    expert_ids,
    route_weight,
    w_experts_in,
    w_experts_out,
    w_shared_in,
    w_shared_out,
    shared_gate,
):
    tok_rows = hidden_in.shape[0]
    width = hidden_in.shape[1]
    head_lanes = lax.axis_size(HEAD)
    device_count = lax.axis_size("tok") * head_lanes
    expert_count = device_count // 2
    top_count = expert_ids.shape[1]
    capacity = 2 * max(1, tok_rows * top_count * 5 // (8 * expert_count))
    normed = lax.all_gather(rms_scale(hidden_in, attn_gain), HEAD, axis=0, tiled=True)
    stretch_rows = normed.shape[0]
    heads_here = proj_weight.shape[2] // HD
    projected = (
        jnp.einsum("td,cdf->ctf", normed, proj_weight, preferred_element_type=jnp.float32)
        + proj_bias.astype(jnp.float32)[:, None, :]
    )
    context = context_len[0]
    positions = context + jnp.arange(stretch_rows, dtype=jnp.int32)
    queries = rotate(projected[0].reshape(stretch_rows, heads_here, HD), positions).astype(
        jnp.bfloat16
    )
    new_keys = rotate(projected[1].reshape(stretch_rows, heads_here, HD), positions).astype(
        jnp.bfloat16
    )
    new_values = projected[2].reshape(stretch_rows, heads_here, HD).astype(jnp.bfloat16)
    ordered = jnp.take(paged_cache, page_table[0], axis=1)
    span_len = ordered.shape[1] * ordered.shape[2]
    ordered = ordered.reshape(2, span_len, heads_here, HD)
    keys_all = jnp.concatenate([ordered[0], new_keys], axis=0)
    values_all = jnp.concatenate([ordered[1], new_values], axis=0)
    part = tok_rows // 2
    query_groups = queries.reshape(head_lanes, 2, part, heads_here, HD)
    pieces = []
    for group in range(2):
        heads_out = attend(
            query_groups[:, group].reshape(head_lanes * part, heads_here, HD),
            keys_all,
            values_all,
            context,
            span_len,
            group,
            part,
        )
        pieces.append(
            lax.psum_scatter(
                jnp.dot(heads_out, out_weight, preferred_element_type=jnp.float32).astype(
                    jnp.bfloat16
                ),
                HEAD,
                scatter_dimension=0,
                tiled=True,
            )
        )
    attn_own = jnp.concatenate(pieces, axis=0).astype(jnp.float32)
    resid = (hidden_in.astype(jnp.float32) + attn_own).astype(jnp.bfloat16)
    mixed = rms_scale(resid, mlp_gain)
    inner = jnp.einsum(
        "td,dcf->tcf",
        lax.all_gather(mixed, HEAD, axis=0, tiled=True),
        w_shared_in,
        preferred_element_type=jnp.float32,
    )
    activated = (jax.nn.silu(inner[:, 0]) * inner[:, 1]).astype(jnp.bfloat16)
    shared_part = jnp.dot(activated, w_shared_out, preferred_element_type=jnp.float32)
    shared_own = lax.psum_scatter(
        shared_part.astype(jnp.bfloat16), HEAD, scatter_dimension=0, tiled=True
    ).astype(jnp.float32)
    gate = jax.nn.sigmoid(jnp.dot(mixed, shared_gate, preferred_element_type=jnp.float32))
    flat_ids = expert_ids.reshape(-1)
    one_hot = (flat_ids[:, None] == jnp.arange(expert_count, dtype=jnp.int32)[None, :]).astype(
        jnp.int32
    )
    earlier = jnp.cumsum(one_hot, axis=0) - one_hot
    slot_pos = jnp.sum(earlier * one_hot, axis=1)
    slot_index = flat_ids * capacity + slot_pos
    slot_table = slot_index.reshape(tok_rows, top_count)
    dispatch_matrix = jnp.sum(
        (
            jnp.arange(expert_count * capacity, dtype=jnp.int32)[:, None, None] == slot_table[None]
        ).astype(jnp.int32),
        axis=2,
    ).astype(jnp.bfloat16)
    buffer = jnp.dot(dispatch_matrix, mixed, preferred_element_type=jnp.float32).astype(
        jnp.bfloat16
    )
    pair = [(0, 1), (1, 0)]
    tiles = (expert_count, capacity, width // 128, 128)
    arrived = lax.all_to_all(buffer.reshape(tiles), ("tok", "x"), 0, 0, tiled=True).reshape(
        expert_count * capacity, width
    )
    sibling = lax.ppermute(arrived, "core", pair)

    def half_expert(rows):
        inner = jnp.dot(rows, w_experts_in[0], preferred_element_type=jnp.float32)
        middle = inner.shape[1] // 2
        activated = (jax.nn.silu(inner[:, :middle]) * inner[:, middle:]).astype(jnp.bfloat16)
        return jnp.dot(activated, w_experts_out[0], preferred_element_type=jnp.float32).astype(
            jnp.bfloat16
        )

    part_own = half_expert(arrived)
    part_back = lax.ppermute(half_expert(sibling), "core", pair)
    merged_own = (part_own.astype(jnp.float32) + part_back.astype(jnp.float32)).astype(
        jnp.bfloat16
    )
    merged = lax.all_to_all(merged_own.reshape(tiles), ("tok", "x"), 0, 0, tiled=True).reshape(
        expert_count * capacity, width
    )
    combine = jnp.sum(
        jnp.where(
            jnp.arange(expert_count * capacity, dtype=jnp.int32)[None, None, :]
            == slot_table[:, :, None],
            route_weight[:, :, None],
            0.0,
        ),
        axis=1,
    )
    routed = jnp.dot(
        combine,
        merged.astype(jnp.float32),
        precision=lax.Precision.HIGHEST,
        preferred_element_type=jnp.float32,
    )
    return (resid.astype(jnp.float32) + gate[:, None] * shared_own + routed).astype(jnp.bfloat16)


def solution(mesh):
    split = Mesh(
        mesh.devices.reshape(mesh.shape["tok"], mesh.shape["head"] // 2, 2), ("tok", "x", "core")
    )
    in_specs = (
        P(ROWS, None),
        P("tok"),
        P("tok", None),
        P(None, "tok", None, HEAD),
        P(),
        P(None, None, HEAD),
        P(None, HEAD),
        P(HEAD, None),
        P(),
        P(ROWS, None),
        P(ROWS, None),
        P(ROWS, None, None),
        P(ROWS, None, None),
        P(None, None, HEAD),
        P(HEAD, None),
        P(),
    )
    out_specs = P(ROWS, None)
    return jax.shard_map(
        per_device, mesh=split, in_specs=in_specs, out_specs=out_specs, check_vma=False
    )
```

```python
import math

import jax
import jax.numpy as jnp
from jax import lax
from jax.experimental import pallas as pl
from jax.experimental.pallas import tpu as pltpu
from jax.sharding import Mesh, PartitionSpec as P

HD = 128
HEAD = ("x", "core")
ROWS = ("tok", "x", "core")


EPS = 1e-06
THETA = 1000000.0


def rms_scale(values, gain):
    wide = values.astype(jnp.float32)
    spread = jnp.mean(wide * wide, axis=-1, keepdims=True)
    return (wide * lax.rsqrt(spread + EPS) * gain.astype(jnp.float32)).astype(jnp.bfloat16)


def rotate(vectors, positions):
    middle = vectors.shape[-1] // 2
    frequency = THETA ** (-(jnp.arange(middle, dtype=jnp.float32) * 2.0 / vectors.shape[-1]))
    angles = positions.astype(jnp.float32)[:, None] * frequency[None, :]
    angles = jnp.concatenate([angles, angles], axis=-1)[:, None, :]
    turned = jnp.concatenate([-vectors[..., middle:], vectors[..., :middle]], axis=-1)
    return vectors * jnp.cos(angles) + turned * jnp.sin(angles)


def attend(queries, keys_all, values_all, context, span_len):
    row_count = queries.shape[0]
    head_count = queries.shape[1]
    head_size = queries.shape[2]
    key_count = keys_all.shape[0]
    block_rows = math.gcd(row_count, 256)
    scale = 1.0 / math.sqrt(head_size)

    def kernel(context_ref, query_ref, key_ref, value_ref, out_ref):
        scores = (
            lax.dot_general(
                query_ref[...],
                key_ref[...],
                (((1,), (1,)), ((), ())),
                preferred_element_type=jnp.float32,
            )
            * scale
        )
        key_pos = lax.broadcasted_iota(jnp.int32, scores.shape, 1)
        query_pos = pl.program_id(1) * block_rows + lax.broadcasted_iota(
            jnp.int32, scores.shape, 0
        )
        cached = key_pos < span_len
        allowed = (cached & (key_pos < context_ref[0])) | (
            jnp.logical_not(cached) & (key_pos - span_len <= query_pos)
        )
        scores = jnp.where(allowed, scores, -1e30)
        largest = jnp.max(scores, axis=-1, keepdims=True)
        weights = jnp.where(allowed, jnp.exp(scores - largest), 0.0)
        probs = (weights / jnp.sum(weights, axis=-1, keepdims=True)).astype(jnp.bfloat16)
        out_ref[...] = jnp.dot(probs, value_ref[...], preferred_element_type=jnp.float32).astype(
            jnp.bfloat16
        )

    width = head_count * head_size
    result = pl.pallas_call(
        kernel,
        out_shape=jax.ShapeDtypeStruct((row_count, width), jnp.bfloat16),
        grid_spec=pltpu.PrefetchScalarGridSpec(
            num_scalar_prefetch=1,
            grid=(head_count, row_count // block_rows),
            in_specs=[
                pl.BlockSpec((block_rows, head_size), lambda h, i, c: (i, h)),
                pl.BlockSpec((key_count, head_size), lambda h, i, c: (0, h)),
                pl.BlockSpec((key_count, head_size), lambda h, i, c: (0, h)),
            ],
            out_specs=pl.BlockSpec((block_rows, head_size), lambda h, i, c: (i, h)),
        ),
    )(
        jnp.reshape(context, (1,)).astype(jnp.int32),
        queries.reshape(row_count, width),
        keys_all.reshape(key_count, width),
        values_all.reshape(key_count, width),
    )
    return result


def per_device(
    hidden_in,
    context_len,
    page_table,
    paged_cache,
    attn_gain,
    proj_weight,
    proj_bias,
    out_weight,
    mlp_gain,
    expert_ids,
    route_weight,
    w_experts_in,
    w_experts_out,
    w_shared_in,
    w_shared_out,
    shared_gate,
):
    tok_rows = hidden_in.shape[0]
    width = hidden_in.shape[1]
    head_lanes = lax.axis_size(HEAD)
    device_count = lax.axis_size("tok") * head_lanes
    expert_count = device_count // 2
    top_count = expert_ids.shape[1]
    capacity = 2 * max(1, tok_rows * top_count * 5 // (8 * expert_count))
    gathered = lax.all_gather(hidden_in, HEAD, axis=0, tiled=True)
    stretch_rows = gathered.shape[0]
    heads_here = proj_weight.shape[2] // HD
    normed = rms_scale(gathered, attn_gain)
    projected = (
        jnp.einsum("td,cdf->ctf", normed, proj_weight, preferred_element_type=jnp.float32)
        + proj_bias.astype(jnp.float32)[:, None, :]
    )
    context = context_len[0]
    positions = context + jnp.arange(stretch_rows, dtype=jnp.int32)
    queries = rotate(projected[0].reshape(stretch_rows, heads_here, HD), positions).astype(
        jnp.bfloat16
    )
    new_keys = rotate(projected[1].reshape(stretch_rows, heads_here, HD), positions).astype(
        jnp.bfloat16
    )
    new_values = projected[2].reshape(stretch_rows, heads_here, HD).astype(jnp.bfloat16)
    ordered = jnp.take(paged_cache, page_table[0], axis=1)
    span_len = ordered.shape[1] * ordered.shape[2]
    ordered = ordered.reshape(2, span_len, heads_here, HD)
    keys_all = jnp.concatenate([ordered[0], new_keys], axis=0)
    values_all = jnp.concatenate([ordered[1], new_values], axis=0)
    heads_out = attend(queries, keys_all, values_all, context, span_len).reshape(
        stretch_rows, heads_here * HD
    )
    attn_all = lax.psum(
        jnp.dot(heads_out, out_weight, preferred_element_type=jnp.float32).astype(jnp.bfloat16),
        HEAD,
    ).astype(jnp.float32)
    resid_all = (gathered.astype(jnp.float32) + attn_all).astype(jnp.bfloat16)
    mixed_all = rms_scale(resid_all, mlp_gain)
    own_start = lax.axis_index(HEAD) * tok_rows
    resid = lax.dynamic_slice_in_dim(resid_all, own_start, tok_rows, axis=0)
    mixed = lax.dynamic_slice_in_dim(mixed_all, own_start, tok_rows, axis=0)
    inner = jnp.einsum(
        "td,dcf->tcf",
        mixed_all,
        w_shared_in,
        preferred_element_type=jnp.float32,
    )
    activated = (jax.nn.silu(inner[:, 0]) * inner[:, 1]).astype(jnp.bfloat16)
    shared_part = jnp.dot(activated, w_shared_out, preferred_element_type=jnp.float32)
    shared_own = lax.psum_scatter(
        shared_part.astype(jnp.bfloat16), HEAD, scatter_dimension=0, tiled=True
    ).astype(jnp.float32)
    gate = jax.nn.sigmoid(jnp.dot(mixed, shared_gate, preferred_element_type=jnp.float32))
    flat_ids = expert_ids.reshape(-1)
    one_hot = (flat_ids[:, None] == jnp.arange(expert_count, dtype=jnp.int32)[None, :]).astype(
        jnp.int32
    )
    earlier = jnp.cumsum(one_hot, axis=0) - one_hot
    slot_pos = jnp.sum(earlier * one_hot, axis=1)
    slot_index = flat_ids * capacity + slot_pos
    slot_table = slot_index.reshape(tok_rows, top_count)
    dispatch_matrix = jnp.sum(
        (
            jnp.arange(expert_count * capacity, dtype=jnp.int32)[:, None, None] == slot_table[None]
        ).astype(jnp.int32),
        axis=2,
    ).astype(jnp.bfloat16)
    buffer = jnp.dot(dispatch_matrix, mixed, preferred_element_type=jnp.float32).astype(
        jnp.bfloat16
    )
    pair = [(0, 1), (1, 0)]
    tiles = (expert_count, capacity, width // 128, 128)
    arrived = lax.all_to_all(buffer.reshape(tiles), ("tok", "x"), 0, 0, tiled=True).reshape(
        expert_count * capacity, width
    )
    sibling = lax.ppermute(arrived, "core", pair)

    def half_expert(rows):
        inner = jnp.dot(rows, w_experts_in[0], preferred_element_type=jnp.float32)
        middle = inner.shape[1] // 2
        activated = (jax.nn.silu(inner[:, :middle]) * inner[:, middle:]).astype(jnp.bfloat16)
        return jnp.dot(activated, w_experts_out[0], preferred_element_type=jnp.float32).astype(
            jnp.bfloat16
        )

    part_own = half_expert(arrived)
    part_back = lax.ppermute(half_expert(sibling), "core", pair)
    merged_own = (part_own.astype(jnp.float32) + part_back.astype(jnp.float32)).astype(
        jnp.bfloat16
    )
    merged = lax.all_to_all(merged_own.reshape(tiles), ("tok", "x"), 0, 0, tiled=True).reshape(
        expert_count * capacity, width
    )
    combine = jnp.sum(
        jnp.where(
            jnp.arange(expert_count * capacity, dtype=jnp.int32)[None, None, :]
            == slot_table[:, :, None],
            route_weight[:, :, None],
            0.0,
        ),
        axis=1,
    )
    routed = jnp.dot(
        combine,
        merged.astype(jnp.float32),
        precision=lax.Precision.HIGHEST,
        preferred_element_type=jnp.float32,
    )
    return (resid.astype(jnp.float32) + gate[:, None] * shared_own + routed).astype(jnp.bfloat16)


def solution(mesh):
    split = Mesh(
        mesh.devices.reshape(mesh.shape["tok"], mesh.shape["head"] // 2, 2), ("tok", "x", "core")
    )
    in_specs = (
        P(ROWS, None),
        P("tok"),
        P("tok", None),
        P(None, "tok", None, HEAD),
        P(),
        P(None, None, HEAD),
        P(None, HEAD),
        P(HEAD, None),
        P(),
        P(ROWS, None),
        P(ROWS, None),
        P(ROWS, None, None),
        P(ROWS, None, None),
        P(None, None, HEAD),
        P(HEAD, None),
        P(),
    )
    out_specs = P(ROWS, None)
    return jax.shard_map(
        per_device, mesh=split, in_specs=in_specs, out_specs=out_specs, check_vma=False
    )
```

```python
import math

import jax
import jax.numpy as jnp
from jax import lax
from jax.experimental import pallas as pl
from jax.experimental.pallas import tpu as pltpu
from jax.sharding import Mesh, PartitionSpec as P

HD = 128
HEAD = ("x", "core")
ROWS = ("tok", "x", "core")


EPS = 1e-06
THETA = 1000000.0


def rms_scale(values, gain):
    wide = values.astype(jnp.float32)
    spread = jnp.mean(wide * wide, axis=-1, keepdims=True)
    return (wide * lax.rsqrt(spread + EPS) * gain.astype(jnp.float32)).astype(jnp.bfloat16)


def rotate(vectors, positions):
    middle = vectors.shape[-1] // 2
    frequency = THETA ** (-(jnp.arange(middle, dtype=jnp.float32) * 2.0 / vectors.shape[-1]))
    angles = positions.astype(jnp.float32)[:, None] * frequency[None, :]
    angles = jnp.concatenate([angles, angles], axis=-1)[:, None, :]
    turned = jnp.concatenate([-vectors[..., middle:], vectors[..., :middle]], axis=-1)
    return vectors * jnp.cos(angles) + turned * jnp.sin(angles)


def attend(queries, keys_all, values_all, context, span_len):
    row_count = queries.shape[0]
    head_count = queries.shape[1]
    head_size = queries.shape[2]
    key_count = keys_all.shape[0]
    block_rows = math.gcd(row_count, 256)
    scale = 1.0 / math.sqrt(head_size)

    def kernel(context_ref, query_ref, key_ref, value_ref, out_ref):
        scores = (
            lax.dot_general(
                query_ref[...],
                key_ref[...],
                (((1,), (1,)), ((), ())),
                preferred_element_type=jnp.float32,
            )
            * scale
        )
        key_pos = lax.broadcasted_iota(jnp.int32, scores.shape, 1)
        query_pos = pl.program_id(1) * block_rows + lax.broadcasted_iota(
            jnp.int32, scores.shape, 0
        )
        cached = key_pos < span_len
        allowed = (cached & (key_pos < context_ref[0])) | (
            jnp.logical_not(cached) & (key_pos - span_len <= query_pos)
        )
        scores = jnp.where(allowed, scores, -1e30)
        largest = jnp.max(scores, axis=-1, keepdims=True)
        weights = jnp.where(allowed, jnp.exp(scores - largest), 0.0)
        probs = (weights / jnp.sum(weights, axis=-1, keepdims=True)).astype(jnp.bfloat16)
        out_ref[...] = jnp.dot(probs, value_ref[...], preferred_element_type=jnp.float32).astype(
            jnp.bfloat16
        )

    width = head_count * head_size
    result = pl.pallas_call(
        kernel,
        out_shape=jax.ShapeDtypeStruct((row_count, width), jnp.bfloat16),
        grid_spec=pltpu.PrefetchScalarGridSpec(
            num_scalar_prefetch=1,
            grid=(head_count, row_count // block_rows),
            in_specs=[
                pl.BlockSpec((block_rows, head_size), lambda h, i, c: (i, h)),
                pl.BlockSpec((key_count, head_size), lambda h, i, c: (0, h)),
                pl.BlockSpec((key_count, head_size), lambda h, i, c: (0, h)),
            ],
            out_specs=pl.BlockSpec((block_rows, head_size), lambda h, i, c: (i, h)),
        ),
    )(
        jnp.reshape(context, (1,)).astype(jnp.int32),
        queries.reshape(row_count, width),
        keys_all.reshape(key_count, width),
        values_all.reshape(key_count, width),
    )
    return result


def per_device(
    hidden_in,
    context_len,
    page_table,
    paged_cache,
    attn_gain,
    proj_weight,
    proj_bias,
    out_weight,
    mlp_gain,
    expert_ids,
    route_weight,
    w_experts_in,
    w_experts_out,
    w_shared_in,
    w_shared_out,
    shared_gate,
):
    tok_rows = hidden_in.shape[0]
    width = hidden_in.shape[1]
    head_lanes = lax.axis_size(HEAD)
    device_count = lax.axis_size("tok") * head_lanes
    expert_count = device_count // 2
    top_count = expert_ids.shape[1]
    capacity = 2 * max(1, tok_rows * top_count * 5 // (8 * expert_count))
    normed = lax.all_gather(rms_scale(hidden_in, attn_gain), HEAD, axis=0, tiled=True)
    stretch_rows = normed.shape[0]
    heads_here = proj_weight.shape[2] // HD
    projected = (
        jnp.einsum("td,cdf->ctf", normed, proj_weight, preferred_element_type=jnp.float32)
        + proj_bias.astype(jnp.float32)[:, None, :]
    )
    context = context_len[0]
    positions = context + jnp.arange(stretch_rows, dtype=jnp.int32)
    queries = rotate(projected[0].reshape(stretch_rows, heads_here, HD), positions).astype(
        jnp.bfloat16
    )
    new_keys = rotate(projected[1].reshape(stretch_rows, heads_here, HD), positions).astype(
        jnp.bfloat16
    )
    new_values = projected[2].reshape(stretch_rows, heads_here, HD).astype(jnp.bfloat16)
    ordered = jnp.take(paged_cache, page_table[0], axis=1)
    span_len = ordered.shape[1] * ordered.shape[2]
    ordered = ordered.reshape(2, span_len, heads_here, HD)
    keys_all = jnp.concatenate([ordered[0], new_keys], axis=0)
    values_all = jnp.concatenate([ordered[1], new_values], axis=0)
    heads_out = attend(queries, keys_all, values_all, context, span_len).reshape(
        stretch_rows, heads_here * HD
    )
    attn_own = lax.psum_scatter(
        jnp.dot(heads_out, out_weight, preferred_element_type=jnp.float32).astype(jnp.bfloat16),
        HEAD,
        scatter_dimension=0,
        tiled=True,
    ).astype(jnp.float32)
    resid = (hidden_in.astype(jnp.float32) + attn_own).astype(jnp.bfloat16)
    mixed = rms_scale(resid, mlp_gain)
    inner = jnp.einsum(
        "td,dcf->tcf",
        lax.all_gather(mixed, HEAD, axis=0, tiled=True),
        w_shared_in,
        preferred_element_type=jnp.float32,
    )
    activated = (jax.nn.silu(inner[:, 0]) * inner[:, 1]).astype(jnp.bfloat16)
    shared_part = jnp.dot(activated, w_shared_out, preferred_element_type=jnp.float32)
    shared_own = lax.psum_scatter(
        shared_part.astype(jnp.bfloat16), HEAD, scatter_dimension=0, tiled=True
    ).astype(jnp.float32)
    gate = jax.nn.sigmoid(jnp.dot(mixed, shared_gate, preferred_element_type=jnp.float32))
    flat_ids = expert_ids.reshape(-1)
    one_hot = (flat_ids[:, None] == jnp.arange(expert_count, dtype=jnp.int32)[None, :]).astype(
        jnp.int32
    )
    earlier = jnp.cumsum(one_hot, axis=0) - one_hot
    slot_pos = jnp.sum(earlier * one_hot, axis=1)
    slot_index = flat_ids * capacity + slot_pos
    slot_table = slot_index.reshape(tok_rows, top_count)
    dispatch_matrix = jnp.sum(
        (
            jnp.arange(expert_count * capacity, dtype=jnp.int32)[:, None, None] == slot_table[None]
        ).astype(jnp.int32),
        axis=2,
    ).astype(jnp.bfloat16)
    buffer = jnp.dot(dispatch_matrix, mixed, preferred_element_type=jnp.float32).astype(
        jnp.bfloat16
    )
    pair = [(0, 1), (1, 0)]
    tiles = (expert_count, capacity, width // 128, 128)
    arrived = lax.all_to_all(buffer.reshape(tiles), ("tok", "x"), 0, 0, tiled=True).reshape(
        expert_count * capacity, width
    )
    sibling = lax.ppermute(arrived, "core", pair)

    def half_expert(rows):
        inner = jnp.dot(rows, w_experts_in[0], preferred_element_type=jnp.float32)
        middle = inner.shape[1] // 2
        activated = (jax.nn.silu(inner[:, :middle]) * inner[:, middle:]).astype(jnp.bfloat16)
        return jnp.dot(activated, w_experts_out[0], preferred_element_type=jnp.float32).astype(
            jnp.bfloat16
        )

    part_own = half_expert(arrived)
    part_back = lax.ppermute(half_expert(sibling), "core", pair)
    merged_own = (part_own.astype(jnp.float32) + part_back.astype(jnp.float32)).astype(
        jnp.bfloat16
    )
    merged = lax.all_to_all(merged_own.reshape(tiles), ("tok", "x"), 0, 0, tiled=True).reshape(
        expert_count * capacity, width
    )
    combine = jnp.sum(
        jnp.where(
            jnp.arange(expert_count * capacity, dtype=jnp.int32)[None, None, :]
            == slot_table[:, :, None],
            route_weight[:, :, None],
            0.0,
        ),
        axis=1,
    )
    routed = jnp.dot(
        combine,
        merged.astype(jnp.float32),
        precision=lax.Precision.HIGHEST,
        preferred_element_type=jnp.float32,
    )
    return (resid.astype(jnp.float32) + gate[:, None] * shared_own + routed).astype(jnp.bfloat16)


def solution(mesh):
    split = Mesh(
        mesh.devices.reshape(mesh.shape["tok"], mesh.shape["head"] // 2, 2), ("tok", "x", "core")
    )
    in_specs = (
        P(ROWS, None),
        P("tok"),
        P("tok", None),
        P(None, "tok", None, HEAD),
        P(),
        P(None, None, HEAD),
        P(None, HEAD),
        P(HEAD, None),
        P(),
        P(ROWS, None),
        P(ROWS, None),
        P(ROWS, None, None),
        P(ROWS, None, None),
        P(None, None, HEAD),
        P(HEAD, None),
        P(),
    )
    out_specs = P(ROWS, None)
    return jax.shard_map(
        per_device, mesh=split, in_specs=in_specs, out_specs=out_specs, check_vma=False
    )
```

```python
import math

import jax
import jax.numpy as jnp
from jax import lax
from jax.experimental import pallas as pl
from jax.experimental.pallas import tpu as pltpu
from jax.sharding import Mesh, PartitionSpec as P

HD = 128
HEAD = ("x", "core")
ROWS = ("tok", "x", "core")


EPS = 1e-06
THETA = 1000000.0


def rms_scale(values, gain):
    wide = values.astype(jnp.float32)
    spread = jnp.mean(wide * wide, axis=-1, keepdims=True)
    return (wide * lax.rsqrt(spread + EPS) * gain.astype(jnp.float32)).astype(jnp.bfloat16)


def rotate(vectors, positions):
    middle = vectors.shape[-1] // 2
    frequency = THETA ** (-(jnp.arange(middle, dtype=jnp.float32) * 2.0 / vectors.shape[-1]))
    angles = positions.astype(jnp.float32)[:, None] * frequency[None, :]
    angles = jnp.concatenate([angles, angles], axis=-1)[:, None, :]
    turned = jnp.concatenate([-vectors[..., middle:], vectors[..., :middle]], axis=-1)
    return vectors * jnp.cos(angles) + turned * jnp.sin(angles)


def attend(queries, keys_all, values_all, context, span_len):
    row_count = queries.shape[0]
    head_count = queries.shape[1]
    head_size = queries.shape[2]
    key_count = keys_all.shape[0]
    block_rows = math.gcd(row_count, 256)
    scale = 1.0 / math.sqrt(head_size)

    def kernel(context_ref, query_ref, key_ref, value_ref, out_ref):
        query = query_ref[...]
        dims = (((1,), (1,)), ((), ()))
        cached_scores = (
            lax.dot_general(
                query, key_ref[:span_len, :], dims, preferred_element_type=jnp.float32
            )
            * scale
        )
        new_scores = (
            lax.dot_general(
                query, key_ref[span_len:, :], dims, preferred_element_type=jnp.float32
            )
            * scale
        )
        cached_pos = lax.broadcasted_iota(jnp.int32, cached_scores.shape, 1)
        cached_scores = jnp.where(cached_pos < context_ref[0], cached_scores, -1e30)
        new_pos = lax.broadcasted_iota(jnp.int32, new_scores.shape, 1)
        query_pos = pl.program_id(1) * block_rows + lax.broadcasted_iota(
            jnp.int32, new_scores.shape, 0
        )
        new_scores = jnp.where(new_pos <= query_pos, new_scores, -1e30)
        largest = jnp.maximum(
            jnp.max(cached_scores, axis=-1, keepdims=True),
            jnp.max(new_scores, axis=-1, keepdims=True),
        )
        cached_weights = jnp.exp(cached_scores - largest)
        new_weights = jnp.exp(new_scores - largest)
        total = jnp.sum(cached_weights, axis=-1, keepdims=True) + jnp.sum(
            new_weights, axis=-1, keepdims=True
        )
        out = jnp.dot(
            (cached_weights / total).astype(jnp.bfloat16),
            value_ref[:span_len, :],
            preferred_element_type=jnp.float32,
        ) + jnp.dot(
            (new_weights / total).astype(jnp.bfloat16),
            value_ref[span_len:, :],
            preferred_element_type=jnp.float32,
        )
        out_ref[...] = out.astype(jnp.bfloat16)

    width = head_count * head_size
    result = pl.pallas_call(
        kernel,
        out_shape=jax.ShapeDtypeStruct((row_count, width), jnp.bfloat16),
        grid_spec=pltpu.PrefetchScalarGridSpec(
            num_scalar_prefetch=1,
            grid=(head_count, row_count // block_rows),
            in_specs=[
                pl.BlockSpec((block_rows, head_size), lambda h, i, c: (i, h)),
                pl.BlockSpec((key_count, head_size), lambda h, i, c: (0, h)),
                pl.BlockSpec((key_count, head_size), lambda h, i, c: (0, h)),
            ],
            out_specs=pl.BlockSpec((block_rows, head_size), lambda h, i, c: (i, h)),
        ),
    )(
        jnp.reshape(context, (1,)).astype(jnp.int32),
        queries.reshape(row_count, width),
        keys_all.reshape(key_count, width),
        values_all.reshape(key_count, width),
    )
    return result


def per_device(
    hidden_in,
    context_len,
    page_table,
    paged_cache,
    attn_gain,
    proj_weight,
    proj_bias,
    out_weight,
    mlp_gain,
    expert_ids,
    route_weight,
    w_experts_in,
    w_experts_out,
    w_shared_in,
    w_shared_out,
    shared_gate,
):
    tok_rows = hidden_in.shape[0]
    width = hidden_in.shape[1]
    head_lanes = lax.axis_size(HEAD)
    device_count = lax.axis_size("tok") * head_lanes
    expert_count = device_count // 2
    top_count = expert_ids.shape[1]
    capacity = 2 * max(1, tok_rows * top_count * 5 // (8 * expert_count))
    normed = lax.all_gather(rms_scale(hidden_in, attn_gain), HEAD, axis=0, tiled=True)
    stretch_rows = normed.shape[0]
    heads_here = proj_weight.shape[2] // HD
    projected = (
        jnp.einsum("td,cdf->ctf", normed, proj_weight, preferred_element_type=jnp.float32)
        + proj_bias.astype(jnp.float32)[:, None, :]
    )
    context = context_len[0]
    positions = context + jnp.arange(stretch_rows, dtype=jnp.int32)
    queries = rotate(projected[0].reshape(stretch_rows, heads_here, HD), positions).astype(
        jnp.bfloat16
    )
    new_keys = rotate(projected[1].reshape(stretch_rows, heads_here, HD), positions).astype(
        jnp.bfloat16
    )
    new_values = projected[2].reshape(stretch_rows, heads_here, HD).astype(jnp.bfloat16)
    ordered = jnp.take(paged_cache, page_table[0], axis=1)
    span_len = ordered.shape[1] * ordered.shape[2]
    ordered = ordered.reshape(2, span_len, heads_here, HD)
    keys_all = jnp.concatenate([ordered[0], new_keys], axis=0)
    values_all = jnp.concatenate([ordered[1], new_values], axis=0)
    heads_out = attend(queries, keys_all, values_all, context, span_len).reshape(
        stretch_rows, heads_here * HD
    )
    attn_own = lax.psum_scatter(
        jnp.dot(heads_out, out_weight, preferred_element_type=jnp.float32).astype(jnp.bfloat16),
        HEAD,
        scatter_dimension=0,
        tiled=True,
    ).astype(jnp.float32)
    resid = (hidden_in.astype(jnp.float32) + attn_own).astype(jnp.bfloat16)
    mixed = rms_scale(resid, mlp_gain)
    inner = jnp.einsum(
        "td,dcf->tcf",
        lax.all_gather(mixed, HEAD, axis=0, tiled=True),
        w_shared_in,
        preferred_element_type=jnp.float32,
    )
    activated = (jax.nn.silu(inner[:, 0]) * inner[:, 1]).astype(jnp.bfloat16)
    shared_part = jnp.dot(activated, w_shared_out, preferred_element_type=jnp.float32)
    shared_own = lax.psum_scatter(
        shared_part.astype(jnp.bfloat16), HEAD, scatter_dimension=0, tiled=True
    ).astype(jnp.float32)
    gate = jax.nn.sigmoid(jnp.dot(mixed, shared_gate, preferred_element_type=jnp.float32))
    flat_ids = expert_ids.reshape(-1)
    one_hot = (flat_ids[:, None] == jnp.arange(expert_count, dtype=jnp.int32)[None, :]).astype(
        jnp.int32
    )
    earlier = jnp.cumsum(one_hot, axis=0) - one_hot
    slot_pos = jnp.sum(earlier * one_hot, axis=1)
    slot_index = flat_ids * capacity + slot_pos
    slot_table = slot_index.reshape(tok_rows, top_count)
    dispatch_matrix = jnp.sum(
        (
            jnp.arange(expert_count * capacity, dtype=jnp.int32)[:, None, None] == slot_table[None]
        ).astype(jnp.int32),
        axis=2,
    ).astype(jnp.bfloat16)
    buffer = jnp.dot(dispatch_matrix, mixed, preferred_element_type=jnp.float32).astype(
        jnp.bfloat16
    )
    pair = [(0, 1), (1, 0)]
    tiles = (expert_count, capacity, width // 128, 128)
    arrived = lax.all_to_all(buffer.reshape(tiles), ("tok", "x"), 0, 0, tiled=True).reshape(
        expert_count * capacity, width
    )
    sibling = lax.ppermute(arrived, "core", pair)

    def half_expert(rows):
        inner = jnp.dot(rows, w_experts_in[0], preferred_element_type=jnp.float32)
        middle = inner.shape[1] // 2
        activated = (jax.nn.silu(inner[:, :middle]) * inner[:, middle:]).astype(jnp.bfloat16)
        return jnp.dot(activated, w_experts_out[0], preferred_element_type=jnp.float32).astype(
            jnp.bfloat16
        )

    part_own = half_expert(arrived)
    part_back = lax.ppermute(half_expert(sibling), "core", pair)
    merged_own = (part_own.astype(jnp.float32) + part_back.astype(jnp.float32)).astype(
        jnp.bfloat16
    )
    merged = lax.all_to_all(merged_own.reshape(tiles), ("tok", "x"), 0, 0, tiled=True).reshape(
        expert_count * capacity, width
    )
    combine = jnp.sum(
        jnp.where(
            jnp.arange(expert_count * capacity, dtype=jnp.int32)[None, None, :]
            == slot_table[:, :, None],
            route_weight[:, :, None],
            0.0,
        ),
        axis=1,
    )
    routed = jnp.dot(
        combine,
        merged.astype(jnp.float32),
        precision=lax.Precision.HIGHEST,
        preferred_element_type=jnp.float32,
    )
    return (resid.astype(jnp.float32) + gate[:, None] * shared_own + routed).astype(jnp.bfloat16)


def solution(mesh):
    split = Mesh(
        mesh.devices.reshape(mesh.shape["tok"], mesh.shape["head"] // 2, 2), ("tok", "x", "core")
    )
    in_specs = (
        P(ROWS, None),
        P("tok"),
        P("tok", None),
        P(None, "tok", None, HEAD),
        P(),
        P(None, None, HEAD),
        P(None, HEAD),
        P(HEAD, None),
        P(),
        P(ROWS, None),
        P(ROWS, None),
        P(ROWS, None, None),
        P(ROWS, None, None),
        P(None, None, HEAD),
        P(HEAD, None),
        P(),
    )
    out_specs = P(ROWS, None)
    return jax.shard_map(
        per_device, mesh=split, in_specs=in_specs, out_specs=out_specs, check_vma=False
    )
```

```python
import math

import jax
import jax.numpy as jnp
from jax import lax
from jax.experimental import pallas as pl
from jax.experimental.pallas import tpu as pltpu
from jax.sharding import Mesh, PartitionSpec as P

HD = 128
HEAD = ("x", "core")
ROWS = ("tok", "x", "core")


EPS = 1e-06
THETA = 1000000.0


def rms_scale(values, gain):
    wide = values.astype(jnp.float32)
    spread = jnp.mean(wide * wide, axis=-1, keepdims=True)
    return (wide * lax.rsqrt(spread + EPS) * gain.astype(jnp.float32)).astype(jnp.bfloat16)


def rotate(vectors, positions):
    middle = vectors.shape[-1] // 2
    frequency = THETA ** (-(jnp.arange(middle, dtype=jnp.float32) * 2.0 / vectors.shape[-1]))
    angles = positions.astype(jnp.float32)[:, None] * frequency[None, :]
    angles = jnp.concatenate([angles, angles], axis=-1)[:, None, :]
    turned = jnp.concatenate([-vectors[..., middle:], vectors[..., :middle]], axis=-1)
    return vectors * jnp.cos(angles) + turned * jnp.sin(angles)


def attend(queries, keys_all, values_all, context, span_len):
    row_count = queries.shape[0]
    head_count = queries.shape[1]
    head_size = queries.shape[2]
    key_count = keys_all.shape[0]
    block_rows = math.gcd(row_count, 512)
    scale = 1.0 / math.sqrt(head_size)

    def kernel(context_ref, query_ref, key_ref, value_ref, out_ref):
        query = query_ref[...]
        dims = (((1,), (1,)), ((), ()))
        cached_scores = (
            lax.dot_general(
                query, key_ref[:span_len, :], dims, preferred_element_type=jnp.float32
            )
            * scale
        )
        new_scores = (
            lax.dot_general(
                query, key_ref[span_len:, :], dims, preferred_element_type=jnp.float32
            )
            * scale
        )
        cached_pos = lax.broadcasted_iota(jnp.int32, cached_scores.shape, 1)
        cached_scores = jnp.where(cached_pos < context_ref[0], cached_scores, -1e30)
        new_pos = lax.broadcasted_iota(jnp.int32, new_scores.shape, 1)
        query_pos = pl.program_id(1) * block_rows + lax.broadcasted_iota(
            jnp.int32, new_scores.shape, 0
        )
        new_scores = jnp.where(new_pos <= query_pos, new_scores, -1e30)
        largest = jnp.maximum(
            jnp.max(cached_scores, axis=-1, keepdims=True),
            jnp.max(new_scores, axis=-1, keepdims=True),
        )
        cached_weights = jnp.exp(cached_scores - largest)
        new_weights = jnp.exp(new_scores - largest)
        total = jnp.sum(cached_weights, axis=-1, keepdims=True) + jnp.sum(
            new_weights, axis=-1, keepdims=True
        )
        out = jnp.dot(
            (cached_weights / total).astype(jnp.bfloat16),
            value_ref[:span_len, :],
            preferred_element_type=jnp.float32,
        ) + jnp.dot(
            (new_weights / total).astype(jnp.bfloat16),
            value_ref[span_len:, :],
            preferred_element_type=jnp.float32,
        )
        out_ref[...] = out.astype(jnp.bfloat16)

    width = head_count * head_size
    result = pl.pallas_call(
        kernel,
        out_shape=jax.ShapeDtypeStruct((row_count, width), jnp.bfloat16),
        grid_spec=pltpu.PrefetchScalarGridSpec(
            num_scalar_prefetch=1,
            grid=(head_count, row_count // block_rows),
            in_specs=[
                pl.BlockSpec((block_rows, head_size), lambda h, i, c: (i, h)),
                pl.BlockSpec((key_count, head_size), lambda h, i, c: (0, h)),
                pl.BlockSpec((key_count, head_size), lambda h, i, c: (0, h)),
            ],
            out_specs=pl.BlockSpec((block_rows, head_size), lambda h, i, c: (i, h)),
        ),
    )(
        jnp.reshape(context, (1,)).astype(jnp.int32),
        queries.reshape(row_count, width),
        keys_all.reshape(key_count, width),
        values_all.reshape(key_count, width),
    )
    return result


def per_device(
    hidden_in,
    context_len,
    page_table,
    paged_cache,
    attn_gain,
    proj_weight,
    proj_bias,
    out_weight,
    mlp_gain,
    expert_ids,
    route_weight,
    w_experts_in,
    w_experts_out,
    w_shared_in,
    w_shared_out,
    shared_gate,
):
    tok_rows = hidden_in.shape[0]
    width = hidden_in.shape[1]
    head_lanes = lax.axis_size(HEAD)
    device_count = lax.axis_size("tok") * head_lanes
    expert_count = device_count // 2
    top_count = expert_ids.shape[1]
    capacity = 2 * max(1, tok_rows * top_count * 5 // (8 * expert_count))
    normed = lax.all_gather(rms_scale(hidden_in, attn_gain), HEAD, axis=0, tiled=True)
    stretch_rows = normed.shape[0]
    heads_here = proj_weight.shape[2] // HD
    projected = (
        jnp.einsum("td,cdf->ctf", normed, proj_weight, preferred_element_type=jnp.float32)
        + proj_bias.astype(jnp.float32)[:, None, :]
    )
    context = context_len[0]
    positions = context + jnp.arange(stretch_rows, dtype=jnp.int32)
    queries = rotate(projected[0].reshape(stretch_rows, heads_here, HD), positions).astype(
        jnp.bfloat16
    )
    new_keys = rotate(projected[1].reshape(stretch_rows, heads_here, HD), positions).astype(
        jnp.bfloat16
    )
    new_values = projected[2].reshape(stretch_rows, heads_here, HD).astype(jnp.bfloat16)
    ordered = jnp.take(paged_cache, page_table[0], axis=1)
    span_len = ordered.shape[1] * ordered.shape[2]
    ordered = ordered.reshape(2, span_len, heads_here, HD)
    keys_all = jnp.concatenate([ordered[0], new_keys], axis=0)
    values_all = jnp.concatenate([ordered[1], new_values], axis=0)
    heads_out = attend(queries, keys_all, values_all, context, span_len).reshape(
        stretch_rows, heads_here * HD
    )
    attn_own = lax.psum_scatter(
        jnp.dot(heads_out, out_weight, preferred_element_type=jnp.float32).astype(jnp.bfloat16),
        HEAD,
        scatter_dimension=0,
        tiled=True,
    ).astype(jnp.float32)
    resid = (hidden_in.astype(jnp.float32) + attn_own).astype(jnp.bfloat16)
    mixed = rms_scale(resid, mlp_gain)
    inner = jnp.einsum(
        "td,dcf->tcf",
        lax.all_gather(mixed, HEAD, axis=0, tiled=True),
        w_shared_in,
        preferred_element_type=jnp.float32,
    )
    activated = (jax.nn.silu(inner[:, 0]) * inner[:, 1]).astype(jnp.bfloat16)
    shared_part = jnp.dot(activated, w_shared_out, preferred_element_type=jnp.float32)
    shared_own = lax.psum_scatter(
        shared_part.astype(jnp.bfloat16), HEAD, scatter_dimension=0, tiled=True
    ).astype(jnp.float32)
    gate = jax.nn.sigmoid(jnp.dot(mixed, shared_gate, preferred_element_type=jnp.float32))
    flat_ids = expert_ids.reshape(-1)
    one_hot = (flat_ids[:, None] == jnp.arange(expert_count, dtype=jnp.int32)[None, :]).astype(
        jnp.int32
    )
    earlier = jnp.cumsum(one_hot, axis=0) - one_hot
    slot_pos = jnp.sum(earlier * one_hot, axis=1)
    slot_index = flat_ids * capacity + slot_pos
    slot_table = slot_index.reshape(tok_rows, top_count)
    dispatch_matrix = jnp.sum(
        (
            jnp.arange(expert_count * capacity, dtype=jnp.int32)[:, None, None] == slot_table[None]
        ).astype(jnp.int32),
        axis=2,
    ).astype(jnp.bfloat16)
    buffer = jnp.dot(dispatch_matrix, mixed, preferred_element_type=jnp.float32).astype(
        jnp.bfloat16
    )
    pair = [(0, 1), (1, 0)]
    tiles = (expert_count, capacity, width // 128, 128)
    arrived = lax.all_to_all(buffer.reshape(tiles), ("tok", "x"), 0, 0, tiled=True).reshape(
        expert_count * capacity, width
    )
    sibling = lax.ppermute(arrived, "core", pair)

    def half_expert(rows):
        inner = jnp.dot(rows, w_experts_in[0], preferred_element_type=jnp.float32)
        middle = inner.shape[1] // 2
        activated = (jax.nn.silu(inner[:, :middle]) * inner[:, middle:]).astype(jnp.bfloat16)
        return jnp.dot(activated, w_experts_out[0], preferred_element_type=jnp.float32).astype(
            jnp.bfloat16
        )

    part_own = half_expert(arrived)
    part_back = lax.ppermute(half_expert(sibling), "core", pair)
    merged_own = (part_own.astype(jnp.float32) + part_back.astype(jnp.float32)).astype(
        jnp.bfloat16
    )
    merged = lax.all_to_all(merged_own.reshape(tiles), ("tok", "x"), 0, 0, tiled=True).reshape(
        expert_count * capacity, width
    )
    combine = jnp.sum(
        jnp.where(
            jnp.arange(expert_count * capacity, dtype=jnp.int32)[None, None, :]
            == slot_table[:, :, None],
            route_weight[:, :, None],
            0.0,
        ),
        axis=1,
    )
    routed = jnp.dot(
        combine,
        merged.astype(jnp.float32),
        precision=lax.Precision.HIGHEST,
        preferred_element_type=jnp.float32,
    )
    return (resid.astype(jnp.float32) + gate[:, None] * shared_own + routed).astype(jnp.bfloat16)


def solution(mesh):
    split = Mesh(
        mesh.devices.reshape(mesh.shape["tok"], mesh.shape["head"] // 2, 2), ("tok", "x", "core")
    )
    in_specs = (
        P(ROWS, None),
        P("tok"),
        P("tok", None),
        P(None, "tok", None, HEAD),
        P(),
        P(None, None, HEAD),
        P(None, HEAD),
        P(HEAD, None),
        P(),
        P(ROWS, None),
        P(ROWS, None),
        P(ROWS, None, None),
        P(ROWS, None, None),
        P(None, None, HEAD),
        P(HEAD, None),
        P(),
    )
    out_specs = P(ROWS, None)
    return jax.shard_map(
        per_device, mesh=split, in_specs=in_specs, out_specs=out_specs, check_vma=False
    )
```

```python
import math

import jax
import jax.numpy as jnp
from jax import lax
from jax.experimental import pallas as pl
from jax.experimental.pallas import tpu as pltpu
from jax.sharding import Mesh, PartitionSpec as P

HD = 128
HEAD = ("x", "core")
ROWS = ("tok", "x", "core")


EPS = 1e-06
THETA = 1000000.0


def rms_scale(values, gain):
    wide = values.astype(jnp.float32)
    spread = jnp.mean(wide * wide, axis=-1, keepdims=True)
    return (wide * lax.rsqrt(spread + EPS) * gain.astype(jnp.float32)).astype(jnp.bfloat16)


def rotate(vectors, positions):
    middle = vectors.shape[-1] // 2
    frequency = THETA ** (-(jnp.arange(middle, dtype=jnp.float32) * 2.0 / vectors.shape[-1]))
    angles = positions.astype(jnp.float32)[:, None] * frequency[None, :]
    angles = jnp.concatenate([angles, angles], axis=-1)[:, None, :]
    turned = jnp.concatenate([-vectors[..., middle:], vectors[..., :middle]], axis=-1)
    return vectors * jnp.cos(angles) + turned * jnp.sin(angles)


def attend(queries, keys_all, values_all, context, span_len):
    row_count = queries.shape[0]
    head_count = queries.shape[1]
    head_size = queries.shape[2]
    key_count = keys_all.shape[0]
    block_rows = math.gcd(row_count, 128)
    scale = 1.0 / math.sqrt(head_size)

    def kernel(context_ref, query_ref, key_ref, value_ref, out_ref):
        query = query_ref[...]
        dims = (((1,), (1,)), ((), ()))
        cached_scores = (
            lax.dot_general(
                query, key_ref[:span_len, :], dims, preferred_element_type=jnp.float32
            )
            * scale
        )
        new_scores = (
            lax.dot_general(
                query, key_ref[span_len:, :], dims, preferred_element_type=jnp.float32
            )
            * scale
        )
        cached_pos = lax.broadcasted_iota(jnp.int32, cached_scores.shape, 1)
        cached_scores = jnp.where(cached_pos < context_ref[0], cached_scores, -1e30)
        new_pos = lax.broadcasted_iota(jnp.int32, new_scores.shape, 1)
        query_pos = pl.program_id(1) * block_rows + lax.broadcasted_iota(
            jnp.int32, new_scores.shape, 0
        )
        new_scores = jnp.where(new_pos <= query_pos, new_scores, -1e30)
        largest = jnp.maximum(
            jnp.max(cached_scores, axis=-1, keepdims=True),
            jnp.max(new_scores, axis=-1, keepdims=True),
        )
        cached_weights = jnp.exp(cached_scores - largest)
        new_weights = jnp.exp(new_scores - largest)
        total = jnp.sum(cached_weights, axis=-1, keepdims=True) + jnp.sum(
            new_weights, axis=-1, keepdims=True
        )
        out = jnp.dot(
            (cached_weights / total).astype(jnp.bfloat16),
            value_ref[:span_len, :],
            preferred_element_type=jnp.float32,
        ) + jnp.dot(
            (new_weights / total).astype(jnp.bfloat16),
            value_ref[span_len:, :],
            preferred_element_type=jnp.float32,
        )
        out_ref[...] = out.astype(jnp.bfloat16)

    width = head_count * head_size
    result = pl.pallas_call(
        kernel,
        out_shape=jax.ShapeDtypeStruct((row_count, width), jnp.bfloat16),
        grid_spec=pltpu.PrefetchScalarGridSpec(
            num_scalar_prefetch=1,
            grid=(head_count, row_count // block_rows),
            in_specs=[
                pl.BlockSpec((block_rows, head_size), lambda h, i, c: (i, h)),
                pl.BlockSpec((key_count, head_size), lambda h, i, c: (0, h)),
                pl.BlockSpec((key_count, head_size), lambda h, i, c: (0, h)),
            ],
            out_specs=pl.BlockSpec((block_rows, head_size), lambda h, i, c: (i, h)),
        ),
    )(
        jnp.reshape(context, (1,)).astype(jnp.int32),
        queries.reshape(row_count, width),
        keys_all.reshape(key_count, width),
        values_all.reshape(key_count, width),
    )
    return result


def per_device(
    hidden_in,
    context_len,
    page_table,
    paged_cache,
    attn_gain,
    proj_weight,
    proj_bias,
    out_weight,
    mlp_gain,
    expert_ids,
    route_weight,
    w_experts_in,
    w_experts_out,
    w_shared_in,
    w_shared_out,
    shared_gate,
):
    tok_rows = hidden_in.shape[0]
    width = hidden_in.shape[1]
    head_lanes = lax.axis_size(HEAD)
    device_count = lax.axis_size("tok") * head_lanes
    expert_count = device_count // 2
    top_count = expert_ids.shape[1]
    capacity = 2 * max(1, tok_rows * top_count * 5 // (8 * expert_count))
    normed = lax.all_gather(rms_scale(hidden_in, attn_gain), HEAD, axis=0, tiled=True)
    stretch_rows = normed.shape[0]
    heads_here = proj_weight.shape[2] // HD
    projected = (
        jnp.einsum("td,cdf->ctf", normed, proj_weight, preferred_element_type=jnp.float32)
        + proj_bias.astype(jnp.float32)[:, None, :]
    )
    context = context_len[0]
    positions = context + jnp.arange(stretch_rows, dtype=jnp.int32)
    queries = rotate(projected[0].reshape(stretch_rows, heads_here, HD), positions).astype(
        jnp.bfloat16
    )
    new_keys = rotate(projected[1].reshape(stretch_rows, heads_here, HD), positions).astype(
        jnp.bfloat16
    )
    new_values = projected[2].reshape(stretch_rows, heads_here, HD).astype(jnp.bfloat16)
    ordered = jnp.take(paged_cache, page_table[0], axis=1)
    span_len = ordered.shape[1] * ordered.shape[2]
    ordered = ordered.reshape(2, span_len, heads_here, HD)
    keys_all = jnp.concatenate([ordered[0], new_keys], axis=0)
    values_all = jnp.concatenate([ordered[1], new_values], axis=0)
    heads_out = attend(queries, keys_all, values_all, context, span_len).reshape(
        stretch_rows, heads_here * HD
    )
    attn_own = lax.psum_scatter(
        jnp.dot(heads_out, out_weight, preferred_element_type=jnp.float32).astype(jnp.bfloat16),
        HEAD,
        scatter_dimension=0,
        tiled=True,
    ).astype(jnp.float32)
    resid = (hidden_in.astype(jnp.float32) + attn_own).astype(jnp.bfloat16)
    mixed = rms_scale(resid, mlp_gain)
    inner = jnp.einsum(
        "td,dcf->tcf",
        lax.all_gather(mixed, HEAD, axis=0, tiled=True),
        w_shared_in,
        preferred_element_type=jnp.float32,
    )
    activated = (jax.nn.silu(inner[:, 0]) * inner[:, 1]).astype(jnp.bfloat16)
    shared_part = jnp.dot(activated, w_shared_out, preferred_element_type=jnp.float32)
    shared_own = lax.psum_scatter(
        shared_part.astype(jnp.bfloat16), HEAD, scatter_dimension=0, tiled=True
    ).astype(jnp.float32)
    gate = jax.nn.sigmoid(jnp.dot(mixed, shared_gate, preferred_element_type=jnp.float32))
    flat_ids = expert_ids.reshape(-1)
    one_hot = (flat_ids[:, None] == jnp.arange(expert_count, dtype=jnp.int32)[None, :]).astype(
        jnp.int32
    )
    earlier = jnp.cumsum(one_hot, axis=0) - one_hot
    slot_pos = jnp.sum(earlier * one_hot, axis=1)
    slot_index = flat_ids * capacity + slot_pos
    slot_table = slot_index.reshape(tok_rows, top_count)
    dispatch_matrix = jnp.sum(
        (
            jnp.arange(expert_count * capacity, dtype=jnp.int32)[:, None, None] == slot_table[None]
        ).astype(jnp.int32),
        axis=2,
    ).astype(jnp.bfloat16)
    buffer = jnp.dot(dispatch_matrix, mixed, preferred_element_type=jnp.float32).astype(
        jnp.bfloat16
    )
    pair = [(0, 1), (1, 0)]
    tiles = (expert_count, capacity, width // 128, 128)
    arrived = lax.all_to_all(buffer.reshape(tiles), ("tok", "x"), 0, 0, tiled=True).reshape(
        expert_count * capacity, width
    )
    sibling = lax.ppermute(arrived, "core", pair)

    def half_expert(rows):
        inner = jnp.dot(rows, w_experts_in[0], preferred_element_type=jnp.float32)
        middle = inner.shape[1] // 2
        activated = (jax.nn.silu(inner[:, :middle]) * inner[:, middle:]).astype(jnp.bfloat16)
        return jnp.dot(activated, w_experts_out[0], preferred_element_type=jnp.float32).astype(
            jnp.bfloat16
        )

    part_own = half_expert(arrived)
    part_back = lax.ppermute(half_expert(sibling), "core", pair)
    merged_own = (part_own.astype(jnp.float32) + part_back.astype(jnp.float32)).astype(
        jnp.bfloat16
    )
    merged = lax.all_to_all(merged_own.reshape(tiles), ("tok", "x"), 0, 0, tiled=True).reshape(
        expert_count * capacity, width
    )
    combine = jnp.sum(
        jnp.where(
            jnp.arange(expert_count * capacity, dtype=jnp.int32)[None, None, :]
            == slot_table[:, :, None],
            route_weight[:, :, None],
            0.0,
        ),
        axis=1,
    )
    routed = jnp.dot(
        combine,
        merged.astype(jnp.float32),
        precision=lax.Precision.HIGHEST,
        preferred_element_type=jnp.float32,
    )
    return (resid.astype(jnp.float32) + gate[:, None] * shared_own + routed).astype(jnp.bfloat16)


def solution(mesh):
    split = Mesh(
        mesh.devices.reshape(mesh.shape["tok"], mesh.shape["head"] // 2, 2), ("tok", "x", "core")
    )
    in_specs = (
        P(ROWS, None),
        P("tok"),
        P("tok", None),
        P(None, "tok", None, HEAD),
        P(),
        P(None, None, HEAD),
        P(None, HEAD),
        P(HEAD, None),
        P(),
        P(ROWS, None),
        P(ROWS, None),
        P(ROWS, None, None),
        P(ROWS, None, None),
        P(None, None, HEAD),
        P(HEAD, None),
        P(),
    )
    out_specs = P(ROWS, None)
    return jax.shard_map(
        per_device, mesh=split, in_specs=in_specs, out_specs=out_specs, check_vma=False
    )
```

```python
import math

import jax
import jax.numpy as jnp
from jax import lax
from jax.experimental import pallas as pl
from jax.experimental.pallas import tpu as pltpu
from jax.sharding import Mesh, PartitionSpec as P

HD = 128
HEAD = ("x", "core")
ROWS = ("tok", "x", "core")


EPS = 1e-06
THETA = 1000000.0


def rms_scale(values, gain):
    wide = values.astype(jnp.float32)
    spread = jnp.mean(wide * wide, axis=-1, keepdims=True)
    return (wide * lax.rsqrt(spread + EPS) * gain.astype(jnp.float32)).astype(jnp.bfloat16)


def rotate(vectors, positions):
    middle = vectors.shape[-1] // 2
    frequency = THETA ** (-(jnp.arange(middle, dtype=jnp.float32) * 2.0 / vectors.shape[-1]))
    angles = positions.astype(jnp.float32)[:, None] * frequency[None, :]
    angles = jnp.concatenate([angles, angles], axis=-1)[:, None, :]
    turned = jnp.concatenate([-vectors[..., middle:], vectors[..., :middle]], axis=-1)
    return vectors * jnp.cos(angles) + turned * jnp.sin(angles)


def attend(queries, keys_all, values_all, context, span_len):
    row_count = queries.shape[0]
    head_count = queries.shape[1]
    head_size = queries.shape[2]
    key_count = keys_all.shape[0]
    block_rows = math.gcd(row_count, 256)
    scale = 1.0 / math.sqrt(head_size)

    def kernel(context_ref, query_ref, key_ref, value_ref, out_ref):
        query = query_ref[...]
        dims = (((1,), (1,)), ((), ()))
        cached_scores = (
            lax.dot_general(
                query, key_ref[:span_len, :], dims, preferred_element_type=jnp.float32
            )
            * scale
        )
        new_scores = (
            lax.dot_general(
                query, key_ref[span_len:, :], dims, preferred_element_type=jnp.float32
            )
            * scale
        )
        cached_pos = lax.broadcasted_iota(jnp.int32, cached_scores.shape, 1)
        cached_scores = jnp.where(cached_pos < context_ref[0], cached_scores, -1e30)
        new_pos = lax.broadcasted_iota(jnp.int32, new_scores.shape, 1)
        query_pos = pl.program_id(1) * block_rows + lax.broadcasted_iota(
            jnp.int32, new_scores.shape, 0
        )
        new_scores = jnp.where(new_pos <= query_pos, new_scores, -1e30)
        largest = jnp.maximum(
            jnp.max(cached_scores, axis=-1, keepdims=True),
            jnp.max(new_scores, axis=-1, keepdims=True),
        )
        cached_weights = jnp.exp(cached_scores - largest)
        new_weights = jnp.exp(new_scores - largest)
        total = 1.0 / (
            jnp.sum(cached_weights, axis=-1, keepdims=True)
            + jnp.sum(new_weights, axis=-1, keepdims=True)
        )
        out = jnp.dot(
            (cached_weights * total).astype(jnp.bfloat16),
            value_ref[:span_len, :],
            preferred_element_type=jnp.float32,
        ) + jnp.dot(
            (new_weights * total).astype(jnp.bfloat16),
            value_ref[span_len:, :],
            preferred_element_type=jnp.float32,
        )
        out_ref[...] = out.astype(jnp.bfloat16)

    width = head_count * head_size
    result = pl.pallas_call(
        kernel,
        out_shape=jax.ShapeDtypeStruct((row_count, width), jnp.bfloat16),
        grid_spec=pltpu.PrefetchScalarGridSpec(
            num_scalar_prefetch=1,
            grid=(head_count, row_count // block_rows),
            in_specs=[
                pl.BlockSpec((block_rows, head_size), lambda h, i, c: (i, h)),
                pl.BlockSpec((key_count, head_size), lambda h, i, c: (0, h)),
                pl.BlockSpec((key_count, head_size), lambda h, i, c: (0, h)),
            ],
            out_specs=pl.BlockSpec((block_rows, head_size), lambda h, i, c: (i, h)),
        ),
    )(
        jnp.reshape(context, (1,)).astype(jnp.int32),
        queries.reshape(row_count, width),
        keys_all.reshape(key_count, width),
        values_all.reshape(key_count, width),
    )
    return result


def per_device(
    hidden_in,
    context_len,
    page_table,
    paged_cache,
    attn_gain,
    proj_weight,
    proj_bias,
    out_weight,
    mlp_gain,
    expert_ids,
    route_weight,
    w_experts_in,
    w_experts_out,
    w_shared_in,
    w_shared_out,
    shared_gate,
):
    tok_rows = hidden_in.shape[0]
    width = hidden_in.shape[1]
    head_lanes = lax.axis_size(HEAD)
    device_count = lax.axis_size("tok") * head_lanes
    expert_count = device_count // 2
    top_count = expert_ids.shape[1]
    capacity = 2 * max(1, tok_rows * top_count * 5 // (8 * expert_count))
    normed = lax.all_gather(rms_scale(hidden_in, attn_gain), HEAD, axis=0, tiled=True)
    stretch_rows = normed.shape[0]
    heads_here = proj_weight.shape[2] // HD
    projected = (
        jnp.einsum("td,cdf->ctf", normed, proj_weight, preferred_element_type=jnp.float32)
        + proj_bias.astype(jnp.float32)[:, None, :]
    )
    context = context_len[0]
    positions = context + jnp.arange(stretch_rows, dtype=jnp.int32)
    queries = rotate(projected[0].reshape(stretch_rows, heads_here, HD), positions).astype(
        jnp.bfloat16
    )
    new_keys = rotate(projected[1].reshape(stretch_rows, heads_here, HD), positions).astype(
        jnp.bfloat16
    )
    new_values = projected[2].reshape(stretch_rows, heads_here, HD).astype(jnp.bfloat16)
    ordered = jnp.take(paged_cache, page_table[0], axis=1)
    span_len = ordered.shape[1] * ordered.shape[2]
    ordered = ordered.reshape(2, span_len, heads_here, HD)
    keys_all = jnp.concatenate([ordered[0], new_keys], axis=0)
    values_all = jnp.concatenate([ordered[1], new_values], axis=0)
    heads_out = attend(queries, keys_all, values_all, context, span_len).reshape(
        stretch_rows, heads_here * HD
    )
    attn_own = lax.psum_scatter(
        jnp.dot(heads_out, out_weight, preferred_element_type=jnp.float32).astype(jnp.bfloat16),
        HEAD,
        scatter_dimension=0,
        tiled=True,
    ).astype(jnp.float32)
    resid = (hidden_in.astype(jnp.float32) + attn_own).astype(jnp.bfloat16)
    mixed = rms_scale(resid, mlp_gain)
    inner = jnp.einsum(
        "td,dcf->tcf",
        lax.all_gather(mixed, HEAD, axis=0, tiled=True),
        w_shared_in,
        preferred_element_type=jnp.float32,
    )
    activated = (jax.nn.silu(inner[:, 0]) * inner[:, 1]).astype(jnp.bfloat16)
    shared_part = jnp.dot(activated, w_shared_out, preferred_element_type=jnp.float32)
    shared_own = lax.psum_scatter(
        shared_part.astype(jnp.bfloat16), HEAD, scatter_dimension=0, tiled=True
    ).astype(jnp.float32)
    gate = jax.nn.sigmoid(jnp.dot(mixed, shared_gate, preferred_element_type=jnp.float32))
    flat_ids = expert_ids.reshape(-1)
    one_hot = (flat_ids[:, None] == jnp.arange(expert_count, dtype=jnp.int32)[None, :]).astype(
        jnp.int32
    )
    earlier = jnp.cumsum(one_hot, axis=0) - one_hot
    slot_pos = jnp.sum(earlier * one_hot, axis=1)
    slot_index = flat_ids * capacity + slot_pos
    slot_table = slot_index.reshape(tok_rows, top_count)
    dispatch_matrix = jnp.sum(
        (
            jnp.arange(expert_count * capacity, dtype=jnp.int32)[:, None, None] == slot_table[None]
        ).astype(jnp.int32),
        axis=2,
    ).astype(jnp.bfloat16)
    buffer = jnp.dot(dispatch_matrix, mixed, preferred_element_type=jnp.float32).astype(
        jnp.bfloat16
    )
    pair = [(0, 1), (1, 0)]
    tiles = (expert_count, capacity, width // 128, 128)
    arrived = lax.all_to_all(buffer.reshape(tiles), ("tok", "x"), 0, 0, tiled=True).reshape(
        expert_count * capacity, width
    )
    sibling = lax.ppermute(arrived, "core", pair)

    def half_expert(rows):
        inner = jnp.dot(rows, w_experts_in[0], preferred_element_type=jnp.float32)
        middle = inner.shape[1] // 2
        activated = (jax.nn.silu(inner[:, :middle]) * inner[:, middle:]).astype(jnp.bfloat16)
        return jnp.dot(activated, w_experts_out[0], preferred_element_type=jnp.float32).astype(
            jnp.bfloat16
        )

    part_own = half_expert(arrived)
    part_back = lax.ppermute(half_expert(sibling), "core", pair)
    merged_own = (part_own.astype(jnp.float32) + part_back.astype(jnp.float32)).astype(
        jnp.bfloat16
    )
    merged = lax.all_to_all(merged_own.reshape(tiles), ("tok", "x"), 0, 0, tiled=True).reshape(
        expert_count * capacity, width
    )
    combine = jnp.sum(
        jnp.where(
            jnp.arange(expert_count * capacity, dtype=jnp.int32)[None, None, :]
            == slot_table[:, :, None],
            route_weight[:, :, None],
            0.0,
        ),
        axis=1,
    )
    routed = jnp.dot(
        combine,
        merged.astype(jnp.float32),
        precision=lax.Precision.HIGHEST,
        preferred_element_type=jnp.float32,
    )
    return (resid.astype(jnp.float32) + gate[:, None] * shared_own + routed).astype(jnp.bfloat16)


def solution(mesh):
    split = Mesh(
        mesh.devices.reshape(mesh.shape["tok"], mesh.shape["head"] // 2, 2), ("tok", "x", "core")
    )
    in_specs = (
        P(ROWS, None),
        P("tok"),
        P("tok", None),
        P(None, "tok", None, HEAD),
        P(),
        P(None, None, HEAD),
        P(None, HEAD),
        P(HEAD, None),
        P(),
        P(ROWS, None),
        P(ROWS, None),
        P(ROWS, None, None),
        P(ROWS, None, None),
        P(None, None, HEAD),
        P(HEAD, None),
        P(),
    )
    out_specs = P(ROWS, None)
    return jax.shard_map(
        per_device, mesh=split, in_specs=in_specs, out_specs=out_specs, check_vma=False
    )
```

```python
import math

import jax
import jax.numpy as jnp
from jax import lax
from jax.experimental import pallas as pl
from jax.experimental.pallas import tpu as pltpu
from jax.sharding import Mesh, PartitionSpec as P

HD = 128
HEAD = ("x", "core")
ROWS = ("tok", "x", "core")


EPS = 1e-06
THETA = 1000000.0


def rms_scale(values, gain):
    wide = values.astype(jnp.float32)
    spread = jnp.mean(wide * wide, axis=-1, keepdims=True)
    return (wide * lax.rsqrt(spread + EPS) * gain.astype(jnp.float32)).astype(jnp.bfloat16)


def rotate(vectors, positions):
    middle = vectors.shape[-1] // 2
    frequency = THETA ** (-(jnp.arange(middle, dtype=jnp.float32) * 2.0 / vectors.shape[-1]))
    angles = positions.astype(jnp.float32)[:, None] * frequency[None, :]
    angles = jnp.concatenate([angles, angles], axis=-1)[:, None, :]
    turned = jnp.concatenate([-vectors[..., middle:], vectors[..., :middle]], axis=-1)
    return vectors * jnp.cos(angles) + turned * jnp.sin(angles)


def attend(queries, keys_all, values_all, context, span_len):
    row_count = queries.shape[0]
    head_count = queries.shape[1]
    head_size = queries.shape[2]
    key_count = keys_all.shape[0]
    block_rows = math.gcd(row_count, 256)
    scale = 1.0 / math.sqrt(head_size)

    def kernel(context_ref, query_ref, key_ref, value_ref, out_ref):
        query = query_ref[...]
        dims = (((1,), (1,)), ((), ()))
        cached_scores = lax.dot_general(
            query, key_ref[:span_len, :], dims, preferred_element_type=jnp.float32
        )
        new_scores = lax.dot_general(
            query, key_ref[span_len:, :], dims, preferred_element_type=jnp.float32
        )
        cached_pos = lax.broadcasted_iota(jnp.int32, cached_scores.shape, 1)
        cached_scores = jnp.where(cached_pos < context_ref[0], cached_scores, -1e30)
        new_pos = lax.broadcasted_iota(jnp.int32, new_scores.shape, 1)
        query_pos = pl.program_id(1) * block_rows + lax.broadcasted_iota(
            jnp.int32, new_scores.shape, 0
        )
        new_scores = jnp.where(new_pos <= query_pos, new_scores, -1e30)
        largest = jnp.maximum(
            jnp.max(cached_scores, axis=-1, keepdims=True),
            jnp.max(new_scores, axis=-1, keepdims=True),
        )
        cached_weights = jnp.exp((cached_scores - largest) * scale)
        new_weights = jnp.exp((new_scores - largest) * scale)
        total = 1.0 / (
            jnp.sum(cached_weights, axis=-1, keepdims=True)
            + jnp.sum(new_weights, axis=-1, keepdims=True)
        )
        out = jnp.dot(
            (cached_weights * total).astype(jnp.bfloat16),
            value_ref[:span_len, :],
            preferred_element_type=jnp.float32,
        ) + jnp.dot(
            (new_weights * total).astype(jnp.bfloat16),
            value_ref[span_len:, :],
            preferred_element_type=jnp.float32,
        )
        out_ref[...] = out.astype(jnp.bfloat16)

    width = head_count * head_size
    result = pl.pallas_call(
        kernel,
        out_shape=jax.ShapeDtypeStruct((row_count, width), jnp.bfloat16),
        grid_spec=pltpu.PrefetchScalarGridSpec(
            num_scalar_prefetch=1,
            grid=(head_count, row_count // block_rows),
            in_specs=[
                pl.BlockSpec((block_rows, head_size), lambda h, i, c: (i, h)),
                pl.BlockSpec((key_count, head_size), lambda h, i, c: (0, h)),
                pl.BlockSpec((key_count, head_size), lambda h, i, c: (0, h)),
            ],
            out_specs=pl.BlockSpec((block_rows, head_size), lambda h, i, c: (i, h)),
        ),
    )(
        jnp.reshape(context, (1,)).astype(jnp.int32),
        queries.reshape(row_count, width),
        keys_all.reshape(key_count, width),
        values_all.reshape(key_count, width),
    )
    return result


def per_device(
    hidden_in,
    context_len,
    page_table,
    paged_cache,
    attn_gain,
    proj_weight,
    proj_bias,
    out_weight,
    mlp_gain,
    expert_ids,
    route_weight,
    w_experts_in,
    w_experts_out,
    w_shared_in,
    w_shared_out,
    shared_gate,
):
    tok_rows = hidden_in.shape[0]
    width = hidden_in.shape[1]
    head_lanes = lax.axis_size(HEAD)
    device_count = lax.axis_size("tok") * head_lanes
    expert_count = device_count // 2
    top_count = expert_ids.shape[1]
    capacity = 2 * max(1, tok_rows * top_count * 5 // (8 * expert_count))
    normed = lax.all_gather(rms_scale(hidden_in, attn_gain), HEAD, axis=0, tiled=True)
    stretch_rows = normed.shape[0]
    heads_here = proj_weight.shape[2] // HD
    projected = (
        jnp.einsum("td,cdf->ctf", normed, proj_weight, preferred_element_type=jnp.float32)
        + proj_bias.astype(jnp.float32)[:, None, :]
    )
    context = context_len[0]
    positions = context + jnp.arange(stretch_rows, dtype=jnp.int32)
    queries = rotate(projected[0].reshape(stretch_rows, heads_here, HD), positions).astype(
        jnp.bfloat16
    )
    new_keys = rotate(projected[1].reshape(stretch_rows, heads_here, HD), positions).astype(
        jnp.bfloat16
    )
    new_values = projected[2].reshape(stretch_rows, heads_here, HD).astype(jnp.bfloat16)
    ordered = jnp.take(paged_cache, page_table[0], axis=1)
    span_len = ordered.shape[1] * ordered.shape[2]
    ordered = ordered.reshape(2, span_len, heads_here, HD)
    keys_all = jnp.concatenate([ordered[0], new_keys], axis=0)
    values_all = jnp.concatenate([ordered[1], new_values], axis=0)
    heads_out = attend(queries, keys_all, values_all, context, span_len).reshape(
        stretch_rows, heads_here * HD
    )
    attn_own = lax.psum_scatter(
        jnp.dot(heads_out, out_weight, preferred_element_type=jnp.float32).astype(jnp.bfloat16),
        HEAD,
        scatter_dimension=0,
        tiled=True,
    ).astype(jnp.float32)
    resid = (hidden_in.astype(jnp.float32) + attn_own).astype(jnp.bfloat16)
    mixed = rms_scale(resid, mlp_gain)
    inner = jnp.einsum(
        "td,dcf->tcf",
        lax.all_gather(mixed, HEAD, axis=0, tiled=True),
        w_shared_in,
        preferred_element_type=jnp.float32,
    )
    activated = (jax.nn.silu(inner[:, 0]) * inner[:, 1]).astype(jnp.bfloat16)
    shared_part = jnp.dot(activated, w_shared_out, preferred_element_type=jnp.float32)
    shared_own = lax.psum_scatter(
        shared_part.astype(jnp.bfloat16), HEAD, scatter_dimension=0, tiled=True
    ).astype(jnp.float32)
    gate = jax.nn.sigmoid(jnp.dot(mixed, shared_gate, preferred_element_type=jnp.float32))
    flat_ids = expert_ids.reshape(-1)
    one_hot = (flat_ids[:, None] == jnp.arange(expert_count, dtype=jnp.int32)[None, :]).astype(
        jnp.int32
    )
    earlier = jnp.cumsum(one_hot, axis=0) - one_hot
    slot_pos = jnp.sum(earlier * one_hot, axis=1)
    slot_index = flat_ids * capacity + slot_pos
    slot_table = slot_index.reshape(tok_rows, top_count)
    dispatch_matrix = jnp.sum(
        (
            jnp.arange(expert_count * capacity, dtype=jnp.int32)[:, None, None] == slot_table[None]
        ).astype(jnp.int32),
        axis=2,
    ).astype(jnp.bfloat16)
    buffer = jnp.dot(dispatch_matrix, mixed, preferred_element_type=jnp.float32).astype(
        jnp.bfloat16
    )
    pair = [(0, 1), (1, 0)]
    tiles = (expert_count, capacity, width // 128, 128)
    arrived = lax.all_to_all(buffer.reshape(tiles), ("tok", "x"), 0, 0, tiled=True).reshape(
        expert_count * capacity, width
    )
    sibling = lax.ppermute(arrived, "core", pair)

    def half_expert(rows):
        inner = jnp.dot(rows, w_experts_in[0], preferred_element_type=jnp.float32)
        middle = inner.shape[1] // 2
        activated = (jax.nn.silu(inner[:, :middle]) * inner[:, middle:]).astype(jnp.bfloat16)
        return jnp.dot(activated, w_experts_out[0], preferred_element_type=jnp.float32).astype(
            jnp.bfloat16
        )

    part_own = half_expert(arrived)
    part_back = lax.ppermute(half_expert(sibling), "core", pair)
    merged_own = (part_own.astype(jnp.float32) + part_back.astype(jnp.float32)).astype(
        jnp.bfloat16
    )
    merged = lax.all_to_all(merged_own.reshape(tiles), ("tok", "x"), 0, 0, tiled=True).reshape(
        expert_count * capacity, width
    )
    combine = jnp.sum(
        jnp.where(
            jnp.arange(expert_count * capacity, dtype=jnp.int32)[None, None, :]
            == slot_table[:, :, None],
            route_weight[:, :, None],
            0.0,
        ),
        axis=1,
    )
    routed = jnp.dot(
        combine,
        merged.astype(jnp.float32),
        precision=lax.Precision.HIGHEST,
        preferred_element_type=jnp.float32,
    )
    return (resid.astype(jnp.float32) + gate[:, None] * shared_own + routed).astype(jnp.bfloat16)


def solution(mesh):
    split = Mesh(
        mesh.devices.reshape(mesh.shape["tok"], mesh.shape["head"] // 2, 2), ("tok", "x", "core")
    )
    in_specs = (
        P(ROWS, None),
        P("tok"),
        P("tok", None),
        P(None, "tok", None, HEAD),
        P(),
        P(None, None, HEAD),
        P(None, HEAD),
        P(HEAD, None),
        P(),
        P(ROWS, None),
        P(ROWS, None),
        P(ROWS, None, None),
        P(ROWS, None, None),
        P(None, None, HEAD),
        P(HEAD, None),
        P(),
    )
    out_specs = P(ROWS, None)
    return jax.shard_map(
        per_device, mesh=split, in_specs=in_specs, out_specs=out_specs, check_vma=False
    )
```
